128 devices in a mesh: wide: 32 (over z, y, core), narrow: 4 (over x).
Axes of the slice: x: 4, y: 4, z: 4, core: 2. Of those that a mesh axis runs over, the one named last changes fastest.
Arguments:
- atm_state: float32 [144, 262144], P(None, ('wide', 'narrow')), may hold values from -6 to 6
- group_owner: int32 [262144, 1], P(('wide', 'narrow')), may hold values from 0 to 127; in each aligned block of 2048 rows (0 to 2047, 2048 to 4095, ...) at most 32 rows name the same one
- regime_ops: bfloat16 [128, 4, 144, 144], P(('wide', 'narrow')), may hold values from -0.5 to 0.5
- flux_map: bfloat16 [144, 4], replicated, may hold values from -0.5 to 0.5
- remap_src: int32 [4, 1024, 1024], P(None, 'wide', 'narrow'), may hold values from 0 to 8
- remap_weight: float32 [4, 1024, 1024], P(None, 'wide', 'narrow'), may hold values from 0.05 to 0.6
- ocean_mask: int32 [1024, 1024], P('wide', 'narrow'), may hold values 0 or 1
- tracer: float32 [62, 1024, 1024], P(None, 'wide', 'narrow'), may hold values from -6 to 6
- surface_height: float32 [1024, 1024], P('wide', 'narrow'), may hold values from -3 to 3
- transports: float32 [2, 1024, 1024], P(None, 'wide', 'narrow'), may hold values from -3 to 3
Outputs:
- atm_new: float32 [144, 262144], P(None, ('wide', 'narrow'))
- tracer_new: float32 [62, 1024, 1024], P(None, 'wide', 'narrow')
- height_new: float32 [1024, 1024], P('wide', 'narrow')
- transports_new: float32 [2, 1024, 1024], P(None, 'wide', 'narrow')
The draws below stay inside these ranges and needn't reach their ends.
Inputs may be any that keep to these rules, and one draw needn't show every extreme that they name: `group_owner`: among the 2048 columns of one device no owner is named more than 32 times, and one is named exactly 32 times.
All inputs are finite; a program needn't handle non-finite values. No bound on the sum of `ocean_mask` on one device may be relied on, other than what follows from the above.
Results may differ from the reference program's by a relative error of at most 0.0043.
Values may be sent and summed in bfloat16 or wider, within the bound.
No kernel may reach another device: no remote copies, remote signals or barrier semaphores. Data moves between devices by JAX's collectives and lax.ppermute only.
A program may use at most 128 MiB of HBM per device.

```python
import math
import jax
import jax.numpy as jnp
import numpy as np
from jax import lax

LO = 62
AR = 16
AC = 128
NPHYS = 4
NSUB = 4
REMAP_K = 4
NFLUX = 4
F = 144
COLS_DEV = 2048
CAP = 32
COLUMNS = 262144
NAR = 512
NAC = 512
NOR = 1024
NOC = 1024
N_NARROW = 4
DEVICES = 128


def with_ends(entries, rng, low, high):
    dims = entries.shape
    index_at = [jax.random.randint(jax.random.fold_in(rng, axis), (), 0, dims[axis]) for axis in range(len(dims))]
    entries = entries.at[tuple(index_at)].set(low)
    longest = dims.index(max(dims))
    index_at[longest] = (index_at[longest] + 1) % dims[longest]
    return entries.at[tuple(index_at)].set(high)


def steps_of(stream_key, dims, cuts, low, high):
    factor_of = 1.0
    for position, shards_of in cuts:
        draws = jax.random.uniform(jax.random.fold_in(jax.random.fold_in(stream_key, 6), position), (shards_of,), jnp.float32, low / len(cuts), high / len(cuts))
        factor_of = factor_of * jnp.repeat(jnp.exp(draws), dims[position] // shards_of).reshape((-1,) + (1,) * (len(dims) - 1 - position))
    return factor_of


def shared_out(stream_key, own, number, rows, number_of, top, bound, lean):
    order = jax.random.permutation(stream_key, number_of)
    crowded, ordinary = shares(number_of, rows * top, bound, lean, True), shares(number_of, rows * top, bound, lean, False)
    places = jnp.arange(number_of)

    def named(sizes, turn):
        used = int((sizes > 0).sum())
        fixed = max(1, used // 4)
        moved = fixed + (places - fixed + turn * (used - fixed)) % max(1, number_of - fixed)
        return jnp.zeros((number_of,), jnp.int32).at[order[jnp.where(places < fixed, places, moved)]].set(jnp.asarray(sizes, jnp.int32))

    sizes = jnp.where(number % 4 == 0, named(crowded, number // 4), named(ordinary, number - number // 4 - 1))
    mixed = jax.random.permutation(jax.random.fold_in(own, 3), number_of)
    donor, receiver = mixed[0:number_of // 2 * 2:2], mixed[1:number_of // 2 * 2:2]
    margin = jnp.minimum(sizes[donor] - 1, bound - sizes[receiver]) // 2
    margin = jnp.where((donor == order[0]) | (receiver == order[0]) | (sizes[receiver] == 0), 0, jnp.maximum(margin, 0))
    moved = jax.random.randint(jax.random.fold_in(own, 4), (number_of // 2,), 0, 1 << 20) % (margin + 1)
    sizes = sizes.at[donor].add(-moved).at[receiver].add(moved)
    items = jnp.searchsorted(jnp.cumsum(sizes), jnp.arange(rows * top), side="right").astype(jnp.int32)
    listing = items.reshape(top, rows).T
    listing = listing[jax.random.permutation(jax.random.fold_in(own, 1), rows)]
    turn = jax.random.randint(jax.random.fold_in(own, 2), (rows, 1), 0, top)
    return jnp.take_along_axis(listing, (jnp.arange(top)[None, :] + turn) % top, axis=1)


def shares(number_of, total, most, skew, full):
    weights = [(1 << 20) // math.isqrt(grade ** skew) + 1 for grade in range(1, number_of + 1)]
    largest = most if full else min(most, max(-(-total // number_of), total * weights[0] // sum(weights)))
    least = 1 if total - largest >= number_of - 1 else 0
    holding, surplus = [largest] + [least] * (number_of - 1), total - largest - least * (number_of - 1)
    while surplus > 0:
        movable = [i for i in range(1, number_of) if holding[i] < largest] or [i for i in range(1, number_of) if holding[i] < most]
        mass, budget = sum([weights[i] for i in movable]), surplus
        for i in movable:
            addition = min(most - holding[i], max(1, budget * weights[i] // mass), surplus)
            holding[i] = holding[i] + addition
            surplus = surplus - addition
    return np.array(holding)


def scatter_about(stream_key, extent, deviation, limit, pieces=(), kind=jnp.bfloat16):
    drawn = jax.random.normal(stream_key, extent, jnp.float32) * deviation
    if len(pieces) > 0:
        drawn = steps_of(stream_key, extent, pieces, -0.22, 0.18) * drawn
    return jnp.clip(drawn, min=-limit, max=limit).astype(kind)


def setup_inputs(seed: int = 0) -> dict:
    key_list = jax.random.split(jax.random.key(seed), 11)
    atm_state = scatter_about(key_list[0], (F, COLUMNS), 1.0, 6.0, ((1, 128),), jnp.float32)
    group_owner_keys = jax.random.split(jax.random.fold_in(key_list[1], 1), COLUMNS // COLS_DEV)
    group_owner_turns = jax.random.permutation(jax.random.fold_in(key_list[1], 3), COLUMNS // COLS_DEV)
    group_owner = jax.vmap(lambda own, number: shared_out(jax.random.fold_in(key_list[1], 2), own, number, COLS_DEV, DEVICES, 1, CAP, 2))(group_owner_keys, group_owner_turns).reshape((COLUMNS, 1))
    regime_ops = scatter_about(key_list[2], (DEVICES, NPHYS, F, F), F ** -0.5, 0.5, ((0, 128),))
    flux_map = scatter_about(key_list[3], (F, NFLUX), F ** -0.5, 0.5)
    remap_src = with_ends(jax.random.randint(key_list[4], (REMAP_K, NOR, NOC), 0, 9), jax.random.fold_in(key_list[4], 1), 0, 8).astype(jnp.int32)
    remap_weight = jnp.clip(jnp.exp(math.log(0.6) - 2.4849067 * jax.random.uniform(key_list[5], (REMAP_K, NOR, NOC), jnp.float32) ** steps_of(key_list[5], (REMAP_K, NOR, NOC), ((1, 32), (2, 4)), -0.2, 0.2)), 0.05, 0.6)
    ocean_mask = with_ends((jax.random.randint(key_list[6], (NOR, NOC), 0, 4) < 3).astype(jnp.int32), jax.random.fold_in(key_list[6], 1), 0, 1)
    tracer = scatter_about(key_list[7], (LO, NOR, NOC), 1.0, 6.0, ((1, 32), (2, 4)), jnp.float32)
    surface_height = scatter_about(key_list[8], (NOR, NOC), 0.5, 3.0, ((0, 32), (1, 4)), jnp.float32)
    transports = scatter_about(key_list[9], (2, NOR, NOC), 0.5, 3.0, ((1, 32), (2, 4)), jnp.float32)
    return dict(atm_state=atm_state, group_owner=group_owner, regime_ops=regime_ops, flux_map=flux_map, remap_src=remap_src, remap_weight=remap_weight, ocean_mask=ocean_mask, tracer=tracer, surface_height=surface_height, transports=transports)


relax_rate = 0.5
kappa_mix = 0.2
heat_gain = 0.5
gravity = 0.7
depth_mean = 0.7
wind_gain = 0.3
fresh_gain = 0.3


def column_ranks(owners, peers):
    onehot = (owners[:, None] == jnp.arange(peers, dtype=jnp.int32)[None, :]).astype(jnp.int32)
    before = jnp.cumsum(onehot, axis=0) - onehot
    return jnp.sum(before * onehot, axis=1)


def physics(operators, columns, flux_map):
    initial = columns.astype(jnp.float32)
    current = initial
    for sweep in range(operators.shape[0]):
        mixed = lax.dot_general(operators[sweep], current.astype(jnp.bfloat16), (((0,), (0,)), ((), ())), preferred_element_type=jnp.float32)
        current = current + relax_rate * jnp.tanh(mixed)
    final = current.astype(jnp.bfloat16)
    tendency = (current - initial).astype(jnp.bfloat16)
    fluxes = lax.dot_general(flux_map, final, (((0,), (0,)), ((), ())), preferred_element_type=jnp.float32).astype(jnp.bfloat16)
    return tendency, fluxes


def diffuse(tracer_ext, mask_ext):
    centre = tracer_ext[:, 1:-1, 1:-1]
    mask_centre = mask_ext[:, 1:-1, 1:-1]
    summed = jnp.zeros_like(centre)
    cuts = ((slice(2, None), slice(1, -1)), (slice(None, -2), slice(1, -1)), (slice(1, -1), slice(2, None)), (slice(1, -1), slice(None, -2)))
    for row_cut, col_cut in cuts:
        summed = summed + mask_centre * mask_ext[:, row_cut, col_cut] * (tracer_ext[:, row_cut, col_cut] - centre)
    return centre + kappa_mix * summed


def momentum(flow, height, height_next, mask, mask_next, stress):
    return mask * mask_next * (flow - gravity * (height_next - height) + wind_gain * stress)


def continuity(height, flow_u, flow_u_west, flow_v, flow_v_south, mask, fresh):
    return mask * (height - depth_mean * ((flow_u - flow_u_west) + (flow_v - flow_v_south)) + fresh_gain * fresh)


def subcycles(height, flow_u, flow_v, mask, forcing, count):
    padded_mask = jnp.pad(mask, 1)
    mask_east = padded_mask[1:-1, 2:]
    mask_north = padded_mask[2:, 1:-1]
    for substep in range(count):
        padded_height = jnp.pad(height, 1)
        flow_u = momentum(flow_u, height, padded_height[1:-1, 2:], mask, mask_east, forcing[1])
        flow_v = momentum(flow_v, height, padded_height[2:, 1:-1], mask, mask_north, forcing[2])
        padded_u = jnp.pad(flow_u, 1)
        padded_v = jnp.pad(flow_v, 1)
        height = continuity(height, flow_u, padded_u[1:-1, :-2], flow_v, padded_v[:-2, 1:-1], mask, forcing[0])
    return height, flow_u, flow_v


def reference(atm_state, group_owner, regime_ops, flux_map, remap_src, remap_weight, ocean_mask, tracer, surface_height, transports):
    owners = group_owner[:, 0]

    def block_ranks(block_owners):
        return column_ranks(block_owners, DEVICES)

    ranks = jax.vmap(block_ranks)(owners.reshape(DEVICES, COLS_DEV)).reshape(-1)
    sources = jnp.arange(COLUMNS, dtype=jnp.int32) // COLS_DEV
    slots = owners * (DEVICES * CAP) + sources * CAP + ranks
    initial = atm_state.astype(jnp.bfloat16)
    buffer = jnp.zeros((F, DEVICES * DEVICES * CAP), jnp.bfloat16).at[:, slots].set(initial)
    per_owner = buffer.reshape(F, DEVICES, DEVICES * CAP).transpose(1, 0, 2)

    def run_owner(pair):
        return physics(pair[0], pair[1], flux_map)

    tendency, fluxes = lax.map(run_owner, (regime_ops, per_owner))
    tend_cols = tendency.transpose(1, 0, 2).reshape(F, -1)[:, slots]
    flux_cols = fluxes.transpose(1, 0, 2).reshape(NFLUX, -1)[:, slots].astype(jnp.float32)
    atm_new = atm_state + tend_cols.astype(jnp.float32)
    rows_here = jnp.arange(NOR, dtype=jnp.int32)[None, :, None] // 2
    cols_here = jnp.arange(NOC, dtype=jnp.int32)[None, None, :] // 2
    atm_row = jnp.clip(rows_here + remap_src // 3 - 1, 0, NAR - 1).astype(jnp.int32)
    atm_col = jnp.clip(cols_here + remap_src % 3 - 1, 0, NAC - 1).astype(jnp.int32)
    source_col = ((atm_row // AR) * N_NARROW + atm_col // AC) * COLS_DEV + (atm_row % AR) * AC + atm_col % AC
    ocean_flux = jnp.sum(flux_cols[:, source_col.astype(jnp.int32)] * remap_weight[None], axis=1)
    mask = ocean_mask.astype(jnp.float32)
    tracer_ext = jnp.pad(tracer, ((0, 0), (1, 1), (1, 1)))
    mask_ext = jnp.pad(mask[None], ((0, 0), (1, 1), (1, 1)))
    tracer_new = diffuse(tracer_ext, mask_ext)
    tracer_new = tracer_new.at[0].add(heat_gain * mask * ocean_flux[0])
    height, flow_u, flow_v = subcycles(surface_height, transports[0], transports[1], mask, ocean_flux[1:], NSUB)
    return atm_new, tracer_new, height, jnp.stack([flow_u, flow_v])
```

```python
import jax
import jax.numpy as jnp
from jax import lax
from jax.sharding import PartitionSpec as P

AC = 128
NSUB = 4
OCEAN_HALO = NSUB
ATM_HALO = OCEAN_HALO // 2 + 1


relax_rate = 0.5
kappa_mix = 0.2
heat_gain = 0.5
gravity = 0.7
depth_mean = 0.7
wind_gain = 0.3
fresh_gain = 0.3


def shift_pairs(count, step):
    return [(i, i + step) for i in range(count) if 0 <= i + step < count]


def with_halo(cells, width):
    wide_count = lax.axis_size("wide")
    narrow_count = lax.axis_size("narrow")
    rows = cells.shape[-2]
    cols = cells.shape[-1]
    above = lax.ppermute(cells[..., rows - width :, :], "wide", shift_pairs(wide_count, 1))
    below = lax.ppermute(cells[..., :width, :], "wide", shift_pairs(wide_count, -1))
    cells = jnp.concatenate([above, cells, below], axis=-2)
    left = lax.ppermute(cells[..., cols - width :], "narrow", shift_pairs(narrow_count, 1))
    right = lax.ppermute(cells[..., :width], "narrow", shift_pairs(narrow_count, -1))
    return jnp.concatenate([left, cells, right], axis=-1)


def plus_halo(cells):
    wide_count = lax.axis_size("wide")
    narrow_count = lax.axis_size("narrow")
    rows = cells.shape[-2]
    cols = cells.shape[-1]
    above = lax.ppermute(cells[..., rows - 1 :, :], "wide", shift_pairs(wide_count, 1))
    below = lax.ppermute(cells[..., :1, :], "wide", shift_pairs(wide_count, -1))
    left = lax.ppermute(cells[..., cols - 1 :], "narrow", shift_pairs(narrow_count, 1))
    right = lax.ppermute(cells[..., :1], "narrow", shift_pairs(narrow_count, -1))
    return above, below, left, right


def column_ranks(owners, peers):
    onehot = (owners[:, None] == jnp.arange(peers, dtype=jnp.int32)[None, :]).astype(jnp.int32)
    before = jnp.cumsum(onehot, axis=0) - onehot
    return jnp.sum(before * onehot, axis=1)


def block_width():
    return 512


def place_columns(source, slots, total):
    width = block_width()
    pieces = []
    for start in range(0, total, width):
        selector = (slots[:, None] == (start + jnp.arange(width, dtype=jnp.int32))[None, :]).astype(
            jnp.bfloat16
        )
        pieces.append(
            jnp.dot(source, selector, preferred_element_type=jnp.float32).astype(jnp.bfloat16)
        )
    return jnp.concatenate(pieces, axis=1)


def fetch_columns(source, slots):
    count = slots.shape[0]
    width = block_width()
    lanes = jnp.arange(source.shape[1], dtype=jnp.int32)
    pieces = []
    for start in range(0, count, width):
        wanted = slots[start : start + width]
        selector = (lanes[:, None] == wanted[None, :]).astype(jnp.bfloat16)
        pieces.append(jnp.dot(source, selector, preferred_element_type=jnp.float32))
    return jnp.concatenate(pieces, axis=1)


def physics(operators, columns, flux_map):
    initial = columns.astype(jnp.float32)
    current = initial
    for sweep in range(operators.shape[0]):
        mixed = lax.dot_general(
            operators[sweep],
            current.astype(jnp.bfloat16),
            (((0,), (0,)), ((), ())),
            preferred_element_type=jnp.float32,
        )
        current = current + relax_rate * jnp.tanh(mixed)
    final = current.astype(jnp.bfloat16)
    tendency = (current - initial).astype(jnp.bfloat16)
    fluxes = lax.dot_general(
        flux_map, final, (((0,), (0,)), ((), ())), preferred_element_type=jnp.float32
    ).astype(jnp.bfloat16)
    return (tendency, fluxes)


def selector(count, origin, offset, limit, base, size):
    fine = origin + jnp.arange(count, dtype=jnp.int32)
    coarse = jnp.clip(fine // 2 + offset, 0, limit - 1) - base
    return (coarse[:, None] == jnp.arange(size, dtype=jnp.int32)[None, :]).astype(jnp.bfloat16)


def remap(flux_ext, src_ext, weight_ext, ocean_rows, ocean_cols, atm_rows, atm_cols):
    nflux = flux_ext.shape[0]
    ext_r = src_ext.shape[1]
    ext_c = src_ext.shape[2]
    block_r = flux_ext.shape[1] - 2 * ATM_HALO
    block_c = flux_ext.shape[2] - 2 * ATM_HALO
    my_wide = lax.axis_index("wide")
    my_narrow = lax.axis_index("narrow")
    row0 = my_wide * ocean_rows - OCEAN_HALO
    col0 = my_narrow * ocean_cols - OCEAN_HALO
    arow0 = my_wide * block_r - ATM_HALO
    acol0 = my_narrow * block_c - ATM_HALO
    col_sel = jnp.concatenate(
        [
            selector(ext_c, col0, dc, atm_cols, acol0, flux_ext.shape[2]).T
            for dc in (-1, 0, 1)
        ],
        axis=1,
    )
    by_cols = jnp.dot(
        flux_ext.reshape(nflux * flux_ext.shape[1], flux_ext.shape[2]),
        col_sel,
        preferred_element_type=jnp.float32,
    ).astype(jnp.bfloat16)
    by_cols = by_cols.reshape(nflux, flux_ext.shape[1], 3 * ext_c)
    ocean_flux = jnp.zeros((nflux, ext_r, ext_c), jnp.float32)
    for dr in (-1, 0, 1):
        row_sel = selector(ext_r, row0, dr, atm_rows, arow0, flux_ext.shape[1])
        shifted = jnp.einsum(
            "ap,fpx->fax", row_sel, by_cols, preferred_element_type=jnp.float32
        )
        for dc in (-1, 0, 1):
            code = (dr + 1) * 3 + (dc + 1)
            weight_sum = jnp.sum(jnp.where(src_ext == code, weight_ext, 0.0), axis=0)
            window = shifted[:, :, (dc + 1) * ext_c : (dc + 2) * ext_c]
            ocean_flux = ocean_flux + weight_sum[None] * window
    return ocean_flux


def diffuse(centre, above, below, left, right, mask, m_above, m_below, m_left, m_right):
    north = jnp.concatenate([centre[:, 1:, :], below], axis=1)
    south = jnp.concatenate([above, centre[:, :-1, :]], axis=1)
    east = jnp.concatenate([centre[:, :, 1:], right], axis=2)
    west = jnp.concatenate([left, centre[:, :, :-1]], axis=2)
    mn = jnp.concatenate([mask[:, 1:, :], m_below], axis=1)
    ms = jnp.concatenate([m_above, mask[:, :-1, :]], axis=1)
    me = jnp.concatenate([mask[:, :, 1:], m_right], axis=2)
    mw = jnp.concatenate([m_left, mask[:, :, :-1]], axis=2)
    summed = jnp.zeros_like(centre)
    for nb, mb in ((north, mn), (south, ms), (east, me), (west, mw)):
        summed = summed + mask * mb * (nb - centre)
    return centre + kappa_mix * summed


def momentum(flow, height, height_next, mask, mask_next, stress):
    return mask * mask_next * (flow - gravity * (height_next - height) + wind_gain * stress)


def continuity(height, flow_u, flow_u_west, flow_v, flow_v_south, mask, fresh):
    return mask * (
        height - depth_mean * (flow_u - flow_u_west + (flow_v - flow_v_south)) + fresh_gain * fresh
    )


def next_col(x):
    return jnp.concatenate([x[:, 1:], jnp.zeros_like(x[:, :1])], axis=1)


def next_row(x):
    return jnp.concatenate([x[1:, :], jnp.zeros_like(x[:1, :])], axis=0)


def prev_col(x):
    return jnp.concatenate([jnp.zeros_like(x[:, :1]), x[:, :-1]], axis=1)


def prev_row(x):
    return jnp.concatenate([jnp.zeros_like(x[:1, :]), x[:-1, :]], axis=0)


def per_device(
    atm_state,
    group_owner,
    regime_ops,
    flux_map,
    remap_src,
    remap_weight,
    ocean_mask,
    tracer,
    surface_height,
    transports,
):
    peers = lax.axis_size(("wide", "narrow"))
    wide_count = lax.axis_size("wide")
    narrow_count = lax.axis_size("narrow")
    features = atm_state.shape[0]
    columns_here = atm_state.shape[1]
    nflux = flux_map.shape[1]
    capacity = 2 * columns_here // peers
    total_slots = peers * capacity
    block_rows = columns_here // AC
    ocean_rows = remap_src.shape[1]
    ocean_cols = remap_src.shape[2]
    kk = remap_src.shape[0]
    h = OCEAN_HALO

    mask = ocean_mask.astype(jnp.float32)
    planes = jnp.concatenate(
        [
            mask[None],
            surface_height[None],
            transports,
            remap_src.astype(jnp.float32),
            remap_weight,
        ],
        axis=0,
    )
    planes_ext = with_halo(planes, h)
    mask_ext = planes_ext[0]
    eta = planes_ext[1]
    flow_u = planes_ext[2]
    flow_v = planes_ext[3]
    src_ext = planes_ext[4 : 4 + kk].astype(jnp.int32)
    weight_ext = planes_ext[4 + kk : 4 + 2 * kk]
    t_above, t_below, t_left, t_right = plus_halo(tracer)
    m_above = mask_ext[None, h - 1 : h, h:-h]
    m_below = mask_ext[None, h + ocean_rows : h + ocean_rows + 1, h:-h]
    m_left = mask_ext[None, h:-h, h - 1 : h]
    m_right = mask_ext[None, h:-h, h + ocean_cols : h + ocean_cols + 1]
    tracer_mixed = diffuse(
        tracer, t_above, t_below, t_left, t_right, mask[None], m_above, m_below, m_left, m_right
    )

    owners = group_owner[:, 0]
    slots = owners * capacity + column_ranks(owners, peers)
    initial = atm_state.astype(jnp.bfloat16)
    outgoing = place_columns(initial, slots, total_slots)
    arrived = lax.all_to_all(outgoing, ("wide", "narrow"), split_axis=1, concat_axis=1, tiled=True)
    tendency, fluxes = physics(regime_ops[0], arrived, flux_map)
    back = lax.all_to_all(
        jnp.concatenate([tendency, fluxes], axis=0),
        ("wide", "narrow"),
        split_axis=1,
        concat_axis=1,
        tiled=True,
    )
    returned = fetch_columns(back, slots)
    tend_cols = returned[:features]
    flux_cols = returned[features:]
    atm_new = atm_state + tend_cols

    flux_block = flux_cols.astype(jnp.bfloat16).reshape(nflux, block_rows, AC)
    flux_ext = with_halo(flux_block, ATM_HALO)
    ocean_flux = remap(
        flux_ext,
        src_ext,
        weight_ext,
        ocean_rows,
        ocean_cols,
        wide_count * block_rows,
        narrow_count * AC,
    )

    inner = (slice(h, h + ocean_rows), slice(h, h + ocean_cols))
    tracer_new = tracer_mixed.at[0].add(heat_gain * mask * ocean_flux[0][inner])

    mask_east = next_col(mask_ext)
    mask_north = next_row(mask_ext)
    for substep in range(NSUB):
        flow_u = momentum(flow_u, eta, next_col(eta), mask_ext, mask_east, ocean_flux[2])
        flow_v = momentum(flow_v, eta, next_row(eta), mask_ext, mask_north, ocean_flux[3])
        eta = continuity(
            eta, flow_u, prev_col(flow_u), flow_v, prev_row(flow_v), mask_ext, ocean_flux[1]
        )
    return (atm_new, tracer_new, eta[inner], jnp.stack([flow_u[inner], flow_v[inner]]))


def solution(mesh):
    in_specs = (
        P(None, ("wide", "narrow")),
        P(("wide", "narrow"), None),
        P(("wide", "narrow"), None, None, None),
        P(),
        P(None, "wide", "narrow"),
        P(None, "wide", "narrow"),
        P("wide", "narrow"),
        P(None, "wide", "narrow"),
        P("wide", "narrow"),
        P(None, "wide", "narrow"),
    )
    out_specs = (
        P(None, ("wide", "narrow")),
        P(None, "wide", "narrow"),
        P("wide", "narrow"),
        P(None, "wide", "narrow"),
    )
    return jax.shard_map(
        per_device, mesh=mesh, in_specs=in_specs, out_specs=out_specs, check_vma=False
    )
```

```python
import jax
import jax.numpy as jnp
from jax import lax
from jax.sharding import PartitionSpec as P

AC = 128
NSUB = 4
OCEAN_HALO = NSUB
ATM_HALO = OCEAN_HALO // 2 + 1


relax_rate = 0.5
kappa_mix = 0.2
heat_gain = 0.5
gravity = 0.7
depth_mean = 0.7
wind_gain = 0.3
fresh_gain = 0.3


def shift_pairs(count, step):
    return [(i, i + step) for i in range(count) if 0 <= i + step < count]


def with_halo(cells, width):
    wide_count = lax.axis_size("wide")
    narrow_count = lax.axis_size("narrow")
    rows = cells.shape[-2]
    cols = cells.shape[-1]
    above = lax.ppermute(cells[..., rows - width :, :], "wide", shift_pairs(wide_count, 1))
    below = lax.ppermute(cells[..., :width, :], "wide", shift_pairs(wide_count, -1))
    cells = jnp.concatenate([above, cells, below], axis=-2)
    left = lax.ppermute(cells[..., cols - width :], "narrow", shift_pairs(narrow_count, 1))
    right = lax.ppermute(cells[..., :width], "narrow", shift_pairs(narrow_count, -1))
    return jnp.concatenate([left, cells, right], axis=-1)


def plus_halo(cells):
    wide_count = lax.axis_size("wide")
    narrow_count = lax.axis_size("narrow")
    rows = cells.shape[-2]
    cols = cells.shape[-1]
    above = lax.ppermute(cells[..., rows - 1 :, :], "wide", shift_pairs(wide_count, 1))
    below = lax.ppermute(cells[..., :1, :], "wide", shift_pairs(wide_count, -1))
    left = lax.ppermute(cells[..., cols - 1 :], "narrow", shift_pairs(narrow_count, 1))
    right = lax.ppermute(cells[..., :1], "narrow", shift_pairs(narrow_count, -1))
    return above, below, left, right


def column_ranks(owners, peers):
    onehot = (owners[:, None] == jnp.arange(peers, dtype=jnp.int32)[None, :]).astype(jnp.int32)
    before = jnp.cumsum(onehot, axis=0) - onehot
    return jnp.sum(before * onehot, axis=1)


def block_width():
    return 512


def place_columns(source, slots, total):
    width = block_width()
    pieces = []
    for start in range(0, total, width):
        selector = ((start + jnp.arange(width, dtype=jnp.int32))[:, None] == slots[None, :]).astype(
            jnp.bfloat16
        )
        pieces.append(
            lax.dot_general(
                selector, source, (((1,), (1,)), ((), ())), preferred_element_type=jnp.float32
            ).astype(jnp.bfloat16)
        )
    return jnp.concatenate(pieces, axis=0)


def physics(operators, columns, flux_map):
    initial = columns.astype(jnp.float32)
    current = initial
    for sweep in range(operators.shape[0]):
        mixed = jnp.dot(
            current.astype(jnp.bfloat16), operators[sweep], preferred_element_type=jnp.float32
        )
        current = current + relax_rate * jnp.tanh(mixed)
    final = current.astype(jnp.bfloat16)
    tendency = (current - initial).astype(jnp.bfloat16)
    fluxes = jnp.dot(final, flux_map, preferred_element_type=jnp.float32).astype(jnp.bfloat16)
    return (tendency, fluxes)


def selector(count, origin, offset, limit, base, size):
    fine = origin + jnp.arange(count, dtype=jnp.int32)
    coarse = jnp.clip(fine // 2 + offset, 0, limit - 1) - base
    return (coarse[:, None] == jnp.arange(size, dtype=jnp.int32)[None, :]).astype(jnp.bfloat16)


def remap(flux_ext, src_ext, weight_ext, ocean_rows, ocean_cols, atm_rows, atm_cols):
    nflux = flux_ext.shape[0]
    ext_r = src_ext.shape[1]
    ext_c = src_ext.shape[2]
    block_r = flux_ext.shape[1] - 2 * ATM_HALO
    block_c = flux_ext.shape[2] - 2 * ATM_HALO
    my_wide = lax.axis_index("wide")
    my_narrow = lax.axis_index("narrow")
    row0 = my_wide * ocean_rows - OCEAN_HALO
    col0 = my_narrow * ocean_cols - OCEAN_HALO
    arow0 = my_wide * block_r - ATM_HALO
    acol0 = my_narrow * block_c - ATM_HALO
    col_sel = jnp.concatenate(
        [
            selector(ext_c, col0, dc, atm_cols, acol0, flux_ext.shape[2]).T
            for dc in (-1, 0, 1)
        ],
        axis=1,
    )
    by_cols = jnp.dot(
        flux_ext.reshape(nflux * flux_ext.shape[1], flux_ext.shape[2]),
        col_sel,
        preferred_element_type=jnp.float32,
    ).astype(jnp.bfloat16)
    by_cols = by_cols.reshape(nflux, flux_ext.shape[1], 3 * ext_c)
    ocean_flux = jnp.zeros((nflux, ext_r, ext_c), jnp.float32)
    for dr in (-1, 0, 1):
        row_sel = selector(ext_r, row0, dr, atm_rows, arow0, flux_ext.shape[1])
        shifted = jnp.einsum(
            "ap,fpx->fax", row_sel, by_cols, preferred_element_type=jnp.float32
        )
        for dc in (-1, 0, 1):
            code = (dr + 1) * 3 + (dc + 1)
            weight_sum = jnp.sum(jnp.where(src_ext == code, weight_ext, 0.0), axis=0)
            window = shifted[:, :, (dc + 1) * ext_c : (dc + 2) * ext_c]
            ocean_flux = ocean_flux + weight_sum[None] * window
    return ocean_flux


def diffuse(centre, above, below, left, right, mask, m_above, m_below, m_left, m_right):
    north = jnp.concatenate([centre[:, 1:, :], below], axis=1)
    south = jnp.concatenate([above, centre[:, :-1, :]], axis=1)
    east = jnp.concatenate([centre[:, :, 1:], right], axis=2)
    west = jnp.concatenate([left, centre[:, :, :-1]], axis=2)
    mn = jnp.concatenate([mask[:, 1:, :], m_below], axis=1)
    ms = jnp.concatenate([m_above, mask[:, :-1, :]], axis=1)
    me = jnp.concatenate([mask[:, :, 1:], m_right], axis=2)
    mw = jnp.concatenate([m_left, mask[:, :, :-1]], axis=2)
    summed = jnp.zeros_like(centre)
    for nb, mb in ((north, mn), (south, ms), (east, me), (west, mw)):
        summed = summed + mask * mb * (nb - centre)
    return centre + kappa_mix * summed


def momentum(flow, height, height_next, mask, mask_next, stress):
    return mask * mask_next * (flow - gravity * (height_next - height) + wind_gain * stress)


def continuity(height, flow_u, flow_u_west, flow_v, flow_v_south, mask, fresh):
    return mask * (
        height - depth_mean * (flow_u - flow_u_west + (flow_v - flow_v_south)) + fresh_gain * fresh
    )


def next_col(x):
    return jnp.concatenate([x[:, 1:], jnp.zeros_like(x[:, :1])], axis=1)


def next_row(x):
    return jnp.concatenate([x[1:, :], jnp.zeros_like(x[:1, :])], axis=0)


def prev_col(x):
    return jnp.concatenate([jnp.zeros_like(x[:, :1]), x[:, :-1]], axis=1)


def prev_row(x):
    return jnp.concatenate([jnp.zeros_like(x[:1, :]), x[:-1, :]], axis=0)


def per_device(
    atm_state,
    group_owner,
    regime_ops,
    flux_map,
    remap_src,
    remap_weight,
    ocean_mask,
    tracer,
    surface_height,
    transports,
):
    peers = lax.axis_size(("wide", "narrow"))
    wide_count = lax.axis_size("wide")
    narrow_count = lax.axis_size("narrow")
    features = atm_state.shape[0]
    columns_here = atm_state.shape[1]
    nflux = flux_map.shape[1]
    capacity = 2 * columns_here // peers
    total_slots = peers * capacity
    block_rows = columns_here // AC
    ocean_rows = remap_src.shape[1]
    ocean_cols = remap_src.shape[2]
    kk = remap_src.shape[0]
    h = OCEAN_HALO

    mask = ocean_mask.astype(jnp.float32)
    planes = jnp.concatenate(
        [
            mask[None],
            surface_height[None],
            transports,
            remap_src.astype(jnp.float32),
            remap_weight,
        ],
        axis=0,
    )
    planes_ext = with_halo(planes, h)
    mask_ext = planes_ext[0]
    eta = planes_ext[1]
    flow_u = planes_ext[2]
    flow_v = planes_ext[3]
    src_ext = planes_ext[4 : 4 + kk].astype(jnp.int32)
    weight_ext = planes_ext[4 + kk : 4 + 2 * kk]
    t_above, t_below, t_left, t_right = plus_halo(tracer)
    m_above = mask_ext[None, h - 1 : h, h:-h]
    m_below = mask_ext[None, h + ocean_rows : h + ocean_rows + 1, h:-h]
    m_left = mask_ext[None, h:-h, h - 1 : h]
    m_right = mask_ext[None, h:-h, h + ocean_cols : h + ocean_cols + 1]
    tracer_mixed = diffuse(
        tracer, t_above, t_below, t_left, t_right, mask[None], m_above, m_below, m_left, m_right
    )

    owners = group_owner[:, 0]
    slots = owners * capacity + column_ranks(owners, peers)
    initial = atm_state.astype(jnp.bfloat16)
    outgoing = place_columns(initial, slots, total_slots)
    arrived = lax.all_to_all(outgoing, ("wide", "narrow"), split_axis=0, concat_axis=0, tiled=True)
    tendency, fluxes = physics(regime_ops[0], arrived, flux_map)
    back = lax.all_to_all(
        jnp.concatenate([tendency, fluxes], axis=1),
        ("wide", "narrow"),
        split_axis=0,
        concat_axis=0,
        tiled=True,
    )
    returned = jnp.take(back, slots, axis=0, mode="clip")
    tend_cols = returned[:, :features].T.astype(jnp.float32)
    flux_cols = returned[:, features:].T
    atm_new = atm_state + tend_cols

    flux_block = flux_cols.astype(jnp.bfloat16).reshape(nflux, block_rows, AC)
    flux_ext = with_halo(flux_block, ATM_HALO)
    ocean_flux = remap(
        flux_ext,
        src_ext,
        weight_ext,
        ocean_rows,
        ocean_cols,
        wide_count * block_rows,
        narrow_count * AC,
    )

    inner = (slice(h, h + ocean_rows), slice(h, h + ocean_cols))
    tracer_new = tracer_mixed.at[0].add(heat_gain * mask * ocean_flux[0][inner])

    mask_east = next_col(mask_ext)
    mask_north = next_row(mask_ext)
    for substep in range(NSUB):
        flow_u = momentum(flow_u, eta, next_col(eta), mask_ext, mask_east, ocean_flux[2])
        flow_v = momentum(flow_v, eta, next_row(eta), mask_ext, mask_north, ocean_flux[3])
        eta = continuity(
            eta, flow_u, prev_col(flow_u), flow_v, prev_row(flow_v), mask_ext, ocean_flux[1]
        )
    return (atm_new, tracer_new, eta[inner], jnp.stack([flow_u[inner], flow_v[inner]]))


def solution(mesh):
    in_specs = (
        P(None, ("wide", "narrow")),
        P(("wide", "narrow"), None),
        P(("wide", "narrow"), None, None, None),
        P(),
        P(None, "wide", "narrow"),
        P(None, "wide", "narrow"),
        P("wide", "narrow"),
        P(None, "wide", "narrow"),
        P("wide", "narrow"),
        P(None, "wide", "narrow"),
    )
    out_specs = (
        P(None, ("wide", "narrow")),
        P(None, "wide", "narrow"),
        P("wide", "narrow"),
        P(None, "wide", "narrow"),
    )
    return jax.shard_map(
        per_device, mesh=mesh, in_specs=in_specs, out_specs=out_specs, check_vma=False
    )
```

```python
import jax
import jax.numpy as jnp
from jax import lax
from jax.sharding import PartitionSpec as P
from jax.experimental import pallas as pl
from jax.experimental.pallas import tpu as pltpu

AC = 128
NSUB = 4
OCEAN_HALO = NSUB
ATM_HALO = OCEAN_HALO // 2 + 1


relax_rate = 0.5
kappa_mix = 0.2
heat_gain = 0.5
gravity = 0.7
depth_mean = 0.7
wind_gain = 0.3
fresh_gain = 0.3


def shift_pairs(count, step):
    return [(i, i + step) for i in range(count) if 0 <= i + step < count]


def with_halo(cells, width):
    wide_count = lax.axis_size("wide")
    narrow_count = lax.axis_size("narrow")
    rows = cells.shape[-2]
    cols = cells.shape[-1]
    above = lax.ppermute(cells[..., rows - width :, :], "wide", shift_pairs(wide_count, 1))
    below = lax.ppermute(cells[..., :width, :], "wide", shift_pairs(wide_count, -1))
    cells = jnp.concatenate([above, cells, below], axis=-2)
    left = lax.ppermute(cells[..., cols - width :], "narrow", shift_pairs(narrow_count, 1))
    right = lax.ppermute(cells[..., :width], "narrow", shift_pairs(narrow_count, -1))
    return jnp.concatenate([left, cells, right], axis=-1)


def plus_halo(cells):
    wide_count = lax.axis_size("wide")
    narrow_count = lax.axis_size("narrow")
    rows = cells.shape[-2]
    cols = cells.shape[-1]
    above = lax.ppermute(cells[:, rows - 1 :, :], "wide", shift_pairs(wide_count, 1))
    below = lax.ppermute(cells[:, :1, :], "wide", shift_pairs(wide_count, -1))
    left = lax.ppermute(cells[:, :, cols - 1], "narrow", shift_pairs(narrow_count, 1))
    right = lax.ppermute(cells[:, :, 0], "narrow", shift_pairs(narrow_count, -1))
    return above, below, left[:, :, None], right[:, :, None]


def column_ranks(owners, peers):
    onehot = (owners[:, None] == jnp.arange(peers, dtype=jnp.int32)[None, :]).astype(jnp.int32)
    before = jnp.cumsum(onehot, axis=0) - onehot
    return jnp.sum(before * onehot, axis=1)


def block_width():
    return 512


def place_columns(source, slots, total):
    width = block_width()
    pieces = []
    for start in range(0, total, width):
        selector = ((start + jnp.arange(width, dtype=jnp.int32))[:, None] == slots[None, :]).astype(
            jnp.bfloat16
        )
        pieces.append(
            lax.dot_general(
                selector, source, (((1,), (1,)), ((), ())), preferred_element_type=jnp.float32
            ).astype(jnp.bfloat16)
        )
    return jnp.concatenate(pieces, axis=0)


def physics_kernel(x_ref, op_ref, fm_ref, out_ref):
    features = x_ref.shape[1]
    initial = x_ref[...].astype(jnp.float32)
    current = initial
    for sweep in range(op_ref.shape[0]):
        mixed = jnp.dot(
            current.astype(jnp.bfloat16), op_ref[sweep], preferred_element_type=jnp.float32
        )
        current = current + relax_rate * jnp.tanh(mixed)
    final = current.astype(jnp.bfloat16)
    out_ref[:, :features] = (current - initial).astype(jnp.bfloat16)
    out_ref[:, features:] = jnp.dot(
        final, fm_ref[...], preferred_element_type=jnp.float32
    ).astype(jnp.bfloat16)


def physics(operators, columns, flux_map):
    slots, features = columns.shape
    nflux = flux_map.shape[1]
    tile = 512
    sweeps = operators.shape[0]
    return pl.pallas_call(
        physics_kernel,
        out_shape=jax.ShapeDtypeStruct((slots, features + nflux), jnp.bfloat16),
        grid=(slots // tile,),
        in_specs=[
            pl.BlockSpec((tile, features), lambda i: (i, 0)),
            pl.BlockSpec((sweeps, features, features), lambda i: (0, 0, 0)),
            pl.BlockSpec((features, nflux), lambda i: (0, 0)),
        ],
        out_specs=pl.BlockSpec((tile, features + nflux), lambda i: (i, 0)),
        cost_estimate=pl.CostEstimate(
            flops=2 * slots * features * (sweeps * features + nflux),
            transcendentals=sweeps * slots * features,
            bytes_accessed=2 * slots * (2 * features + nflux) + 2 * sweeps * features * features,
        ),
    )(columns, operators, flux_map)


def selector(count, origin, offset, limit, base, size):
    fine = origin + jnp.arange(count, dtype=jnp.int32)
    coarse = jnp.clip(fine // 2 + offset, 0, limit - 1) - base
    return (coarse[:, None] == jnp.arange(size, dtype=jnp.int32)[None, :]).astype(jnp.bfloat16)


def remap(flux_ext, src_ext, weight_ext, ocean_rows, ocean_cols, atm_rows, atm_cols):
    nflux = flux_ext.shape[0]
    ext_r = src_ext.shape[1]
    ext_c = src_ext.shape[2]
    block_r = flux_ext.shape[1] - 2 * ATM_HALO
    block_c = flux_ext.shape[2] - 2 * ATM_HALO
    my_wide = lax.axis_index("wide")
    my_narrow = lax.axis_index("narrow")
    row0 = my_wide * ocean_rows - OCEAN_HALO
    col0 = my_narrow * ocean_cols - OCEAN_HALO
    arow0 = my_wide * block_r - ATM_HALO
    acol0 = my_narrow * block_c - ATM_HALO
    col_sel = jnp.concatenate(
        [
            selector(ext_c, col0, dc, atm_cols, acol0, flux_ext.shape[2]).T
            for dc in (-1, 0, 1)
        ],
        axis=1,
    )
    by_cols = jnp.dot(
        flux_ext.reshape(nflux * flux_ext.shape[1], flux_ext.shape[2]),
        col_sel,
        preferred_element_type=jnp.float32,
    ).astype(jnp.bfloat16)
    by_cols = by_cols.reshape(nflux, flux_ext.shape[1], 3 * ext_c)
    ocean_flux = jnp.zeros((nflux, ext_r, ext_c), jnp.float32)
    for dr in (-1, 0, 1):
        row_sel = selector(ext_r, row0, dr, atm_rows, arow0, flux_ext.shape[1])
        shifted = jnp.einsum(
            "ap,fpx->fax", row_sel, by_cols, preferred_element_type=jnp.float32
        )
        for dc in (-1, 0, 1):
            code = (dr + 1) * 3 + (dc + 1)
            weight_sum = jnp.sum(jnp.where(src_ext == code, weight_ext, 0.0), axis=0)
            window = shifted[:, :, (dc + 1) * ext_c : (dc + 2) * ext_c]
            ocean_flux = ocean_flux + weight_sum[None] * window
    return ocean_flux


def diffuse(centre, above, below, left, right, mask, m_above, m_below, m_left, m_right):
    north = jnp.concatenate([centre[:, 1:, :], below], axis=1)
    south = jnp.concatenate([above, centre[:, :-1, :]], axis=1)
    east = jnp.concatenate([centre[:, :, 1:], right], axis=2)
    west = jnp.concatenate([left, centre[:, :, :-1]], axis=2)
    mn = jnp.concatenate([mask[:, 1:, :], m_below], axis=1)
    ms = jnp.concatenate([m_above, mask[:, :-1, :]], axis=1)
    me = jnp.concatenate([mask[:, :, 1:], m_right], axis=2)
    mw = jnp.concatenate([m_left, mask[:, :, :-1]], axis=2)
    summed = jnp.zeros_like(centre)
    for nb, mb in ((north, mn), (south, ms), (east, me), (west, mw)):
        summed = summed + mask * mb * (nb - centre)
    return centre + kappa_mix * summed


def momentum(flow, height, height_next, mask, mask_next, stress):
    return mask * mask_next * (flow - gravity * (height_next - height) + wind_gain * stress)


def continuity(height, flow_u, flow_u_west, flow_v, flow_v_south, mask, fresh):
    return mask * (
        height - depth_mean * (flow_u - flow_u_west + (flow_v - flow_v_south)) + fresh_gain * fresh
    )


def next_col(x):
    return jnp.concatenate([x[:, 1:], jnp.zeros_like(x[:, :1])], axis=1)


def next_row(x):
    return jnp.concatenate([x[1:, :], jnp.zeros_like(x[:1, :])], axis=0)


def prev_col(x):
    return jnp.concatenate([jnp.zeros_like(x[:, :1]), x[:, :-1]], axis=1)


def prev_row(x):
    return jnp.concatenate([jnp.zeros_like(x[:1, :]), x[:-1, :]], axis=0)


def per_device(
    atm_state,
    group_owner,
    regime_ops,
    flux_map,
    remap_src,
    remap_weight,
    ocean_mask,
    tracer,
    surface_height,
    transports,
):
    peers = lax.axis_size(("wide", "narrow"))
    wide_count = lax.axis_size("wide")
    narrow_count = lax.axis_size("narrow")
    features = atm_state.shape[0]
    columns_here = atm_state.shape[1]
    nflux = flux_map.shape[1]
    capacity = 2 * columns_here // peers
    total_slots = peers * capacity
    block_rows = columns_here // AC
    ocean_rows = remap_src.shape[1]
    ocean_cols = remap_src.shape[2]
    kk = remap_src.shape[0]
    h = OCEAN_HALO

    mask = ocean_mask.astype(jnp.float32)
    planes = jnp.concatenate(
        [
            mask[None],
            surface_height[None],
            transports,
            remap_src.astype(jnp.float32),
            remap_weight,
        ],
        axis=0,
    )
    planes_ext = with_halo(planes, h)
    mask_ext = planes_ext[0]
    eta = planes_ext[1]
    flow_u = planes_ext[2]
    flow_v = planes_ext[3]
    src_ext = planes_ext[4 : 4 + kk].astype(jnp.int32)
    weight_ext = planes_ext[4 + kk : 4 + 2 * kk]
    t_above, t_below, t_left, t_right = plus_halo(tracer)
    m_above = mask_ext[None, h - 1 : h, h:-h]
    m_below = mask_ext[None, h + ocean_rows : h + ocean_rows + 1, h:-h]
    m_left = mask_ext[None, h:-h, h - 1 : h]
    m_right = mask_ext[None, h:-h, h + ocean_cols : h + ocean_cols + 1]
    tracer_mixed = diffuse(
        tracer, t_above, t_below, t_left, t_right, mask[None], m_above, m_below, m_left, m_right
    )

    owners = group_owner[:, 0]
    slots = owners * capacity + column_ranks(owners, peers)
    initial = atm_state.astype(jnp.bfloat16)
    outgoing = place_columns(initial, slots, total_slots)
    arrived = lax.all_to_all(outgoing, ("wide", "narrow"), split_axis=0, concat_axis=0, tiled=True)
    back = lax.all_to_all(
        physics(regime_ops[0], arrived, flux_map),
        ("wide", "narrow"),
        split_axis=0,
        concat_axis=0,
        tiled=True,
    )
    returned = jnp.take(back, slots, axis=0, mode="clip")
    tend_cols = returned[:, :features].T.astype(jnp.float32)
    flux_cols = returned[:, features:].T
    atm_new = atm_state + tend_cols

    flux_block = flux_cols.astype(jnp.bfloat16).reshape(nflux, block_rows, AC)
    flux_ext = with_halo(flux_block, ATM_HALO)
    ocean_flux = remap(
        flux_ext,
        src_ext,
        weight_ext,
        ocean_rows,
        ocean_cols,
        wide_count * block_rows,
        narrow_count * AC,
    )

    inner = (slice(h, h + ocean_rows), slice(h, h + ocean_cols))
    tracer_new = tracer_mixed.at[0].add(heat_gain * mask * ocean_flux[0][inner])

    mask_east = next_col(mask_ext)
    mask_north = next_row(mask_ext)
    for substep in range(NSUB):
        flow_u = momentum(flow_u, eta, next_col(eta), mask_ext, mask_east, ocean_flux[2])
        flow_v = momentum(flow_v, eta, next_row(eta), mask_ext, mask_north, ocean_flux[3])
        eta = continuity(
            eta, flow_u, prev_col(flow_u), flow_v, prev_row(flow_v), mask_ext, ocean_flux[1]
        )
    return (atm_new, tracer_new, eta[inner], jnp.stack([flow_u[inner], flow_v[inner]]))


def solution(mesh):
    in_specs = (
        P(None, ("wide", "narrow")),
        P(("wide", "narrow"), None),
        P(("wide", "narrow"), None, None, None),
        P(),
        P(None, "wide", "narrow"),
        P(None, "wide", "narrow"),
        P("wide", "narrow"),
        P(None, "wide", "narrow"),
        P("wide", "narrow"),
        P(None, "wide", "narrow"),
    )
    out_specs = (
        P(None, ("wide", "narrow")),
        P(None, "wide", "narrow"),
        P("wide", "narrow"),
        P(None, "wide", "narrow"),
    )
    return jax.shard_map(
        per_device, mesh=mesh, in_specs=in_specs, out_specs=out_specs, check_vma=False
    )
```

```python
import jax
import jax.numpy as jnp
from jax import lax
from jax.sharding import PartitionSpec as P
from jax.experimental import pallas as pl
from jax.experimental.pallas import tpu as pltpu

AC = 128
NSUB = 4
OCEAN_HALO = NSUB
ATM_HALO = OCEAN_HALO // 2 + 1


relax_rate = 0.5
kappa_mix = 0.2
heat_gain = 0.5
gravity = 0.7
depth_mean = 0.7
wind_gain = 0.3
fresh_gain = 0.3


def shift_pairs(count, step):
    return [(i, i + step) for i in range(count) if 0 <= i + step < count]


def with_halo(cells, width):
    wide_count = lax.axis_size("wide")
    narrow_count = lax.axis_size("narrow")
    rows = cells.shape[-2]
    cols = cells.shape[-1]
    above = lax.ppermute(cells[..., rows - width :, :], "wide", shift_pairs(wide_count, 1))
    below = lax.ppermute(cells[..., :width, :], "wide", shift_pairs(wide_count, -1))
    cells = jnp.concatenate([above, cells, below], axis=-2)
    left = lax.ppermute(cells[..., cols - width :], "narrow", shift_pairs(narrow_count, 1))
    right = lax.ppermute(cells[..., :width], "narrow", shift_pairs(narrow_count, -1))
    return jnp.concatenate([left, cells, right], axis=-1)


def with_halo_once(cells, width):
    wide_count = lax.axis_size("wide")
    narrow_count = lax.axis_size("narrow")
    both = ("wide", "narrow")
    rows = cells.shape[-2]
    cols = cells.shape[-1]
    h = width

    def diagonal(dw, dn):
        return [
            (w * narrow_count + n, (w + dw) * narrow_count + n + dn)
            for w in range(wide_count)
            for n in range(narrow_count)
            if 0 <= w + dw < wide_count and 0 <= n + dn < narrow_count
        ]

    first_rows = cells[..., :h, :]
    last_rows = cells[..., rows - h :, :]
    above = lax.ppermute(last_rows, "wide", shift_pairs(wide_count, 1))
    below = lax.ppermute(first_rows, "wide", shift_pairs(wide_count, -1))
    left = lax.ppermute(cells[..., cols - h :], "narrow", shift_pairs(narrow_count, 1))
    right = lax.ppermute(cells[..., :h], "narrow", shift_pairs(narrow_count, -1))
    above_left = lax.ppermute(last_rows[..., cols - h :], both, diagonal(1, 1))
    above_right = lax.ppermute(last_rows[..., :h], both, diagonal(1, -1))
    below_left = lax.ppermute(first_rows[..., cols - h :], both, diagonal(-1, 1))
    below_right = lax.ppermute(first_rows[..., :h], both, diagonal(-1, -1))
    top = jnp.concatenate([above_left, above, above_right], axis=-1)
    middle = jnp.concatenate([left, cells, right], axis=-1)
    bottom = jnp.concatenate([below_left, below, below_right], axis=-1)
    return jnp.concatenate([top, middle, bottom], axis=-2)


def plus_halo(cells):
    wide_count = lax.axis_size("wide")
    narrow_count = lax.axis_size("narrow")
    rows = cells.shape[-2]
    cols = cells.shape[-1]
    above = lax.ppermute(cells[:, rows - 1 :, :], "wide", shift_pairs(wide_count, 1))
    below = lax.ppermute(cells[:, :1, :], "wide", shift_pairs(wide_count, -1))
    left = lax.ppermute(cells[:, :, cols - 1], "narrow", shift_pairs(narrow_count, 1))
    right = lax.ppermute(cells[:, :, 0], "narrow", shift_pairs(narrow_count, -1))
    return above, below, left[:, :, None], right[:, :, None]


def column_ranks(owners, peers):
    onehot = (owners[:, None] == jnp.arange(peers, dtype=jnp.int32)[None, :]).astype(jnp.int32)
    before = jnp.cumsum(onehot, axis=0) - onehot
    return jnp.sum(before * onehot, axis=1)


def block_width():
    return 512


def place_columns(source, slots, total):
    width = block_width()
    pieces = []
    for start in range(0, total, width):
        selector = ((start + jnp.arange(width, dtype=jnp.int32))[:, None] == slots[None, :]).astype(
            jnp.bfloat16
        )
        pieces.append(
            lax.dot_general(
                selector, source, (((1,), (1,)), ((), ())), preferred_element_type=jnp.float32
            ).astype(jnp.bfloat16)
        )
    return jnp.concatenate(pieces, axis=0)


def physics_kernel(x_ref, op_ref, fm_ref, out_ref):
    features = x_ref.shape[1]
    initial = x_ref[...].astype(jnp.float32)
    current = initial
    for sweep in range(op_ref.shape[0]):
        mixed = jnp.dot(
            current.astype(jnp.bfloat16), op_ref[sweep], preferred_element_type=jnp.float32
        )
        current = current + relax_rate * jnp.tanh(mixed)
    final = current.astype(jnp.bfloat16)
    out_ref[:, :features] = (current - initial).astype(jnp.bfloat16)
    out_ref[:, features:] = jnp.dot(
        final, fm_ref[...], preferred_element_type=jnp.float32
    ).astype(jnp.bfloat16)


def physics(operators, columns, flux_map):
    slots, features = columns.shape
    nflux = flux_map.shape[1]
    tile = min(slots, 2048)
    sweeps = operators.shape[0]
    return pl.pallas_call(
        physics_kernel,
        out_shape=jax.ShapeDtypeStruct((slots, features + nflux), jnp.bfloat16),
        grid=(slots // tile,),
        in_specs=[
            pl.BlockSpec((tile, features), lambda i: (i, 0)),
            pl.BlockSpec((sweeps, features, features), lambda i: (0, 0, 0)),
            pl.BlockSpec((features, nflux), lambda i: (0, 0)),
        ],
        out_specs=pl.BlockSpec((tile, features + nflux), lambda i: (i, 0)),
        cost_estimate=pl.CostEstimate(
            flops=2 * slots * features * (sweeps * features + nflux),
            transcendentals=sweeps * slots * features,
            bytes_accessed=2 * slots * (2 * features + nflux) + 2 * sweeps * features * features,
        ),
    )(columns, operators, flux_map)


def unpack_kernel(got_ref, atm_ref, eye_ref, atm_out_ref, flux_out_ref):
    features = atm_ref.shape[0]
    turned = lax.dot_general(
        eye_ref[...], got_ref[...], (((1,), (1,)), ((), ())), preferred_element_type=jnp.float32
    )
    atm_out_ref[...] = atm_ref[...] + turned[:features]
    flux_out_ref[...] = turned[features:].astype(flux_out_ref.dtype)


def unpack(got, atm_state):
    columns, width = got.shape
    features = atm_state.shape[0]
    tile = min(columns, 512)
    eye = jnp.eye(width, dtype=jnp.bfloat16)
    return pl.pallas_call(
        unpack_kernel,
        out_shape=(
            jax.ShapeDtypeStruct((features, columns), jnp.float32),
            jax.ShapeDtypeStruct((width - features, columns), jnp.bfloat16),
        ),
        grid=(columns // tile,),
        in_specs=[
            pl.BlockSpec((tile, width), lambda i: (i, 0)),
            pl.BlockSpec((features, tile), lambda i: (0, i)),
            pl.BlockSpec((width, width), lambda i: (0, 0)),
        ],
        out_specs=(
            pl.BlockSpec((features, tile), lambda i: (0, i)),
            pl.BlockSpec((width - features, tile), lambda i: (0, i)),
        ),
        cost_estimate=pl.CostEstimate(
            flops=2 * columns * width * width,
            transcendentals=0,
            bytes_accessed=2 * columns * width + 8 * columns * features + 2 * columns * width,
        ),
    )(got, atm_state, eye)


def selector(count, origin, offset, limit, base, size):
    fine = origin + jnp.arange(count, dtype=jnp.int32)
    coarse = jnp.clip(fine // 2 + offset, 0, limit - 1) - base
    return (coarse[:, None] == jnp.arange(size, dtype=jnp.int32)[None, :]).astype(jnp.bfloat16)


def remap(flux_ext, src_ext, weight_ext, ocean_rows, ocean_cols, atm_rows, atm_cols):
    nflux = flux_ext.shape[0]
    ext_r = src_ext.shape[1]
    ext_c = src_ext.shape[2]
    block_r = flux_ext.shape[1] - 2 * ATM_HALO
    block_c = flux_ext.shape[2] - 2 * ATM_HALO
    my_wide = lax.axis_index("wide")
    my_narrow = lax.axis_index("narrow")
    row0 = my_wide * ocean_rows - OCEAN_HALO
    col0 = my_narrow * ocean_cols - OCEAN_HALO
    arow0 = my_wide * block_r - ATM_HALO
    acol0 = my_narrow * block_c - ATM_HALO
    col_sel = jnp.concatenate(
        [
            selector(ext_c, col0, dc, atm_cols, acol0, flux_ext.shape[2]).T
            for dc in (-1, 0, 1)
        ],
        axis=1,
    )
    by_cols = jnp.dot(
        flux_ext.reshape(nflux * flux_ext.shape[1], flux_ext.shape[2]),
        col_sel,
        preferred_element_type=jnp.float32,
    ).astype(jnp.bfloat16)
    by_cols = by_cols.reshape(nflux, flux_ext.shape[1], 3 * ext_c)
    ocean_flux = jnp.zeros((nflux, ext_r, ext_c), jnp.float32)
    for dr in (-1, 0, 1):
        row_sel = selector(ext_r, row0, dr, atm_rows, arow0, flux_ext.shape[1])
        shifted = jnp.einsum(
            "ap,fpx->fax", row_sel, by_cols, preferred_element_type=jnp.float32
        )
        for dc in (-1, 0, 1):
            code = (dr + 1) * 3 + (dc + 1)
            weight_sum = jnp.sum(jnp.where(src_ext == code, weight_ext, 0.0), axis=0)
            window = shifted[:, :, (dc + 1) * ext_c : (dc + 2) * ext_c]
            ocean_flux = ocean_flux + weight_sum[None] * window
    return ocean_flux


def diffuse(centre, above, below, left, right, mask, m_above, m_below, m_left, m_right):
    north = jnp.concatenate([centre[:, 1:, :], below], axis=1)
    south = jnp.concatenate([above, centre[:, :-1, :]], axis=1)
    east = jnp.concatenate([centre[:, :, 1:], right], axis=2)
    west = jnp.concatenate([left, centre[:, :, :-1]], axis=2)
    mn = jnp.concatenate([mask[:, 1:, :], m_below], axis=1)
    ms = jnp.concatenate([m_above, mask[:, :-1, :]], axis=1)
    me = jnp.concatenate([mask[:, :, 1:], m_right], axis=2)
    mw = jnp.concatenate([m_left, mask[:, :, :-1]], axis=2)
    summed = jnp.zeros_like(centre)
    for nb, mb in ((north, mn), (south, ms), (east, me), (west, mw)):
        summed = summed + mask * mb * (nb - centre)
    return centre + kappa_mix * summed


def momentum(flow, height, height_next, mask, mask_next, stress):
    return mask * mask_next * (flow - gravity * (height_next - height) + wind_gain * stress)


def continuity(height, flow_u, flow_u_west, flow_v, flow_v_south, mask, fresh):
    return mask * (
        height - depth_mean * (flow_u - flow_u_west + (flow_v - flow_v_south)) + fresh_gain * fresh
    )


def next_col(x):
    return jnp.concatenate([x[:, 1:], jnp.zeros_like(x[:, :1])], axis=1)


def next_row(x):
    return jnp.concatenate([x[1:, :], jnp.zeros_like(x[:1, :])], axis=0)


def prev_col(x):
    return jnp.concatenate([jnp.zeros_like(x[:, :1]), x[:, :-1]], axis=1)


def prev_row(x):
    return jnp.concatenate([jnp.zeros_like(x[:1, :]), x[:-1, :]], axis=0)


def per_device(
    atm_state,
    group_owner,
    regime_ops,
    flux_map,
    remap_src,
    remap_weight,
    ocean_mask,
    tracer,
    surface_height,
    transports,
):
    peers = lax.axis_size(("wide", "narrow"))
    wide_count = lax.axis_size("wide")
    narrow_count = lax.axis_size("narrow")
    features = atm_state.shape[0]
    columns_here = atm_state.shape[1]
    nflux = flux_map.shape[1]
    capacity = 2 * columns_here // peers
    total_slots = peers * capacity
    block_rows = columns_here // AC
    ocean_rows = remap_src.shape[1]
    ocean_cols = remap_src.shape[2]
    kk = remap_src.shape[0]
    h = OCEAN_HALO

    mask = ocean_mask.astype(jnp.float32)
    planes = jnp.concatenate(
        [
            mask[None],
            surface_height[None],
            transports,
            remap_src.astype(jnp.float32),
            remap_weight,
        ],
        axis=0,
    )
    planes_ext = with_halo(planes, h)
    mask_ext = planes_ext[0]
    eta = planes_ext[1]
    flow_u = planes_ext[2]
    flow_v = planes_ext[3]
    src_ext = planes_ext[4 : 4 + kk].astype(jnp.int32)
    weight_ext = planes_ext[4 + kk : 4 + 2 * kk]
    t_above, t_below, t_left, t_right = plus_halo(tracer)
    m_above = mask_ext[None, h - 1 : h, h:-h]
    m_below = mask_ext[None, h + ocean_rows : h + ocean_rows + 1, h:-h]
    m_left = mask_ext[None, h:-h, h - 1 : h]
    m_right = mask_ext[None, h:-h, h + ocean_cols : h + ocean_cols + 1]
    tracer_mixed = diffuse(
        tracer, t_above, t_below, t_left, t_right, mask[None], m_above, m_below, m_left, m_right
    )

    owners = group_owner[:, 0]
    slots = owners * capacity + column_ranks(owners, peers)
    initial = atm_state.astype(jnp.bfloat16)
    outgoing = place_columns(initial, slots, total_slots)
    arrived = lax.all_to_all(outgoing, ("wide", "narrow"), split_axis=0, concat_axis=0, tiled=True)
    back = lax.all_to_all(
        physics(regime_ops[0], arrived, flux_map),
        ("wide", "narrow"),
        split_axis=0,
        concat_axis=0,
        tiled=True,
    )
    returned = jnp.take(back, slots, axis=0, mode="clip")
    atm_new, flux_cols = unpack(returned, atm_state)

    flux_block = flux_cols.astype(jnp.bfloat16).reshape(nflux, block_rows, AC)
    flux_ext = with_halo_once(flux_block, ATM_HALO)
    ocean_flux = remap(
        flux_ext,
        src_ext,
        weight_ext,
        ocean_rows,
        ocean_cols,
        wide_count * block_rows,
        narrow_count * AC,
    )

    inner = (slice(h, h + ocean_rows), slice(h, h + ocean_cols))
    tracer_new = tracer_mixed.at[0].add(heat_gain * mask * ocean_flux[0][inner])

    mask_east = next_col(mask_ext)
    mask_north = next_row(mask_ext)
    for substep in range(NSUB):
        flow_u = momentum(flow_u, eta, next_col(eta), mask_ext, mask_east, ocean_flux[2])
        flow_v = momentum(flow_v, eta, next_row(eta), mask_ext, mask_north, ocean_flux[3])
        eta = continuity(
            eta, flow_u, prev_col(flow_u), flow_v, prev_row(flow_v), mask_ext, ocean_flux[1]
        )
    return (atm_new, tracer_new, eta[inner], jnp.stack([flow_u[inner], flow_v[inner]]))


def solution(mesh):
    in_specs = (
        P(None, ("wide", "narrow")),
        P(("wide", "narrow"), None),
        P(("wide", "narrow"), None, None, None),
        P(),
        P(None, "wide", "narrow"),
        P(None, "wide", "narrow"),
        P("wide", "narrow"),
        P(None, "wide", "narrow"),
        P("wide", "narrow"),
        P(None, "wide", "narrow"),
    )
    out_specs = (
        P(None, ("wide", "narrow")),
        P(None, "wide", "narrow"),
        P("wide", "narrow"),
        P(None, "wide", "narrow"),
    )
    return jax.shard_map(
        per_device, mesh=mesh, in_specs=in_specs, out_specs=out_specs, check_vma=False
    )
```

```python
import jax
import jax.numpy as jnp
from jax import lax
from jax.sharding import PartitionSpec as P
from jax.experimental import pallas as pl

AC = 128
NSUB = 4
OCEAN_HALO = NSUB
ATM_HALO = OCEAN_HALO // 2 + 1


relax_rate = 0.5
kappa_mix = 0.2
heat_gain = 0.5
gravity = 0.7
depth_mean = 0.7
wind_gain = 0.3
fresh_gain = 0.3


def shift_pairs(count, step):
    return [(i, i + step) for i in range(count) if 0 <= i + step < count]


def with_halo(cells, width):
    wide_count = lax.axis_size("wide")
    narrow_count = lax.axis_size("narrow")
    rows = cells.shape[-2]
    cols = cells.shape[-1]
    above = lax.ppermute(cells[..., rows - width :, :], "wide", shift_pairs(wide_count, 1))
    below = lax.ppermute(cells[..., :width, :], "wide", shift_pairs(wide_count, -1))
    cells = jnp.concatenate([above, cells, below], axis=-2)
    left = lax.ppermute(cells[..., cols - width :], "narrow", shift_pairs(narrow_count, 1))
    right = lax.ppermute(cells[..., :width], "narrow", shift_pairs(narrow_count, -1))
    return jnp.concatenate([left, cells, right], axis=-1)


def plus_halo(cells):
    wide_count = lax.axis_size("wide")
    narrow_count = lax.axis_size("narrow")
    rows = cells.shape[-2]
    cols = cells.shape[-1]
    above = lax.ppermute(cells[:, rows - 1 :, :], "wide", shift_pairs(wide_count, 1))
    below = lax.ppermute(cells[:, :1, :], "wide", shift_pairs(wide_count, -1))
    left = lax.ppermute(cells[:, :, cols - 1], "narrow", shift_pairs(narrow_count, 1))
    right = lax.ppermute(cells[:, :, 0], "narrow", shift_pairs(narrow_count, -1))
    return above, below, left[:, :, None], right[:, :, None]


def column_ranks(owners, peers):
    onehot = (owners[:, None] == jnp.arange(peers, dtype=jnp.int32)[None, :]).astype(jnp.int32)
    before = jnp.cumsum(onehot, axis=0) - onehot
    return jnp.sum(before * onehot, axis=1)


def block_width():
    return 512


def place_columns(source, slots, total):
    width = block_width()
    pieces = []
    for start in range(0, total, width):
        selector = ((start + jnp.arange(width, dtype=jnp.int32))[:, None] == slots[None, :]).astype(
            jnp.bfloat16
        )
        pieces.append(
            lax.dot_general(
                selector, source, (((1,), (1,)), ((), ())), preferred_element_type=jnp.float32
            ).astype(jnp.bfloat16)
        )
    return jnp.concatenate(pieces, axis=0)


def physics_kernel(x_ref, op_ref, fm_ref, out_ref):
    features = x_ref.shape[1]
    initial = x_ref[...].astype(jnp.float32)
    current = initial
    for sweep in range(op_ref.shape[0]):
        mixed = jnp.dot(
            current.astype(jnp.bfloat16), op_ref[sweep], preferred_element_type=jnp.float32
        )
        current = current + relax_rate * jnp.tanh(mixed)
    final = current.astype(jnp.bfloat16)
    out_ref[:, :features] = (current - initial).astype(jnp.bfloat16)
    out_ref[:, features:] = jnp.dot(
        final, fm_ref[...], preferred_element_type=jnp.float32
    ).astype(jnp.bfloat16)


def physics(operators, columns, flux_map):
    slots, features = columns.shape
    nflux = flux_map.shape[1]
    tile = min(slots, 2048)
    sweeps = operators.shape[0]
    return pl.pallas_call(
        physics_kernel,
        out_shape=jax.ShapeDtypeStruct((slots, features + nflux), jnp.bfloat16),
        grid=(slots // tile,),
        in_specs=[
            pl.BlockSpec((tile, features), lambda i: (i, 0)),
            pl.BlockSpec((sweeps, features, features), lambda i: (0, 0, 0)),
            pl.BlockSpec((features, nflux), lambda i: (0, 0)),
        ],
        out_specs=pl.BlockSpec((tile, features + nflux), lambda i: (i, 0)),
        cost_estimate=pl.CostEstimate(
            flops=2 * slots * features * (sweeps * features + nflux),
            transcendentals=sweeps * slots * features,
            bytes_accessed=2 * slots * (2 * features + nflux) + 2 * sweeps * features * features,
        ),
    )(columns, operators, flux_map)


def unpack_kernel(got_ref, atm_ref, eye_ref, atm_out_ref, flux_out_ref):
    features = atm_ref.shape[0]
    turned = lax.dot_general(
        eye_ref[...], got_ref[...], (((1,), (1,)), ((), ())), preferred_element_type=jnp.float32
    )
    atm_out_ref[...] = atm_ref[...] + turned[:features]
    flux_out_ref[...] = turned[features:].astype(flux_out_ref.dtype)


def unpack(got, atm_state):
    columns, width = got.shape
    features = atm_state.shape[0]
    tile = min(columns, 512)
    eye = jnp.eye(width, dtype=jnp.bfloat16)
    return pl.pallas_call(
        unpack_kernel,
        out_shape=(
            jax.ShapeDtypeStruct((features, columns), jnp.float32),
            jax.ShapeDtypeStruct((width - features, columns), jnp.bfloat16),
        ),
        grid=(columns // tile,),
        in_specs=[
            pl.BlockSpec((tile, width), lambda i: (i, 0)),
            pl.BlockSpec((features, tile), lambda i: (0, i)),
            pl.BlockSpec((width, width), lambda i: (0, 0)),
        ],
        out_specs=(
            pl.BlockSpec((features, tile), lambda i: (0, i)),
            pl.BlockSpec((width - features, tile), lambda i: (0, i)),
        ),
        cost_estimate=pl.CostEstimate(
            flops=2 * columns * width * width,
            transcendentals=0,
            bytes_accessed=2 * columns * width + 8 * columns * features + 2 * columns * width,
        ),
    )(got, atm_state, eye)


def selector(count, origin, offset, limit, base, size):
    fine = origin + jnp.arange(count, dtype=jnp.int32)
    coarse = jnp.clip(fine // 2 + offset, 0, limit - 1) - base
    return (coarse[:, None] == jnp.arange(size, dtype=jnp.int32)[None, :]).astype(jnp.bfloat16)


def remap(flux_ext, src_ext, weight_ext, ocean_rows, ocean_cols, atm_rows, atm_cols):
    nflux = flux_ext.shape[0]
    ext_r = src_ext.shape[1]
    ext_c = src_ext.shape[2]
    block_r = flux_ext.shape[1] - 2 * ATM_HALO
    block_c = flux_ext.shape[2] - 2 * ATM_HALO
    my_wide = lax.axis_index("wide")
    my_narrow = lax.axis_index("narrow")
    row0 = my_wide * ocean_rows - OCEAN_HALO
    col0 = my_narrow * ocean_cols - OCEAN_HALO
    arow0 = my_wide * block_r - ATM_HALO
    acol0 = my_narrow * block_c - ATM_HALO
    col_sel = jnp.concatenate(
        [
            selector(ext_c, col0, dc, atm_cols, acol0, flux_ext.shape[2]).T
            for dc in (-1, 0, 1)
        ],
        axis=1,
    )
    by_cols = jnp.dot(
        flux_ext.reshape(nflux * flux_ext.shape[1], flux_ext.shape[2]),
        col_sel,
        preferred_element_type=jnp.float32,
    ).astype(jnp.bfloat16)
    by_cols = by_cols.reshape(nflux, flux_ext.shape[1], 3 * ext_c)
    ocean_flux = jnp.zeros((nflux, ext_r, ext_c), jnp.float32)
    for dr in (-1, 0, 1):
        row_sel = selector(ext_r, row0, dr, atm_rows, arow0, flux_ext.shape[1])
        shifted = jnp.einsum(
            "ap,fpx->fax", row_sel, by_cols, preferred_element_type=jnp.float32
        )
        for dc in (-1, 0, 1):
            code = (dr + 1) * 3 + (dc + 1)
            weight_sum = jnp.sum(jnp.where(src_ext == code, weight_ext, 0.0), axis=0)
            window = shifted[:, :, (dc + 1) * ext_c : (dc + 2) * ext_c]
            ocean_flux = ocean_flux + weight_sum[None] * window
    return ocean_flux


def diffuse(centre, above, below, left, right, mask, m_above, m_below, m_left, m_right):
    north = jnp.concatenate([centre[:, 1:, :], below], axis=1)
    south = jnp.concatenate([above, centre[:, :-1, :]], axis=1)
    east = jnp.concatenate([centre[:, :, 1:], right], axis=2)
    west = jnp.concatenate([left, centre[:, :, :-1]], axis=2)
    mn = jnp.concatenate([mask[:, 1:, :], m_below], axis=1)
    ms = jnp.concatenate([m_above, mask[:, :-1, :]], axis=1)
    me = jnp.concatenate([mask[:, :, 1:], m_right], axis=2)
    mw = jnp.concatenate([m_left, mask[:, :, :-1]], axis=2)
    summed = jnp.zeros_like(centre)
    for nb, mb in ((north, mn), (south, ms), (east, me), (west, mw)):
        summed = summed + mask * mb * (nb - centre)
    return centre + kappa_mix * summed


def momentum(flow, height, height_next, mask, mask_next, stress):
    return mask * mask_next * (flow - gravity * (height_next - height) + wind_gain * stress)


def continuity(height, flow_u, flow_u_west, flow_v, flow_v_south, mask, fresh):
    return mask * (
        height - depth_mean * (flow_u - flow_u_west + (flow_v - flow_v_south)) + fresh_gain * fresh
    )


def next_col(x):
    return jnp.concatenate([x[:, 1:], jnp.zeros_like(x[:, :1])], axis=1)


def next_row(x):
    return jnp.concatenate([x[1:, :], jnp.zeros_like(x[:1, :])], axis=0)


def prev_col(x):
    return jnp.concatenate([jnp.zeros_like(x[:, :1]), x[:, :-1]], axis=1)


def prev_row(x):
    return jnp.concatenate([jnp.zeros_like(x[:1, :]), x[:-1, :]], axis=0)


def per_device(
    atm_state,
    group_owner,
    regime_ops,
    flux_map,
    remap_src,
    remap_weight,
    ocean_mask,
    tracer,
    surface_height,
    transports,
):
    peers = lax.axis_size(("wide", "narrow"))
    wide_count = lax.axis_size("wide")
    narrow_count = lax.axis_size("narrow")
    columns_here = atm_state.shape[1]
    nflux = flux_map.shape[1]
    capacity = 2 * columns_here // peers
    total_slots = peers * capacity
    block_rows = columns_here // AC
    ocean_rows = remap_src.shape[1]
    ocean_cols = remap_src.shape[2]
    kk = remap_src.shape[0]
    h = OCEAN_HALO

    mask = ocean_mask.astype(jnp.float32)
    planes = jnp.concatenate(
        [
            mask[None],
            surface_height[None],
            transports,
            remap_src.astype(jnp.float32),
            remap_weight,
        ],
        axis=0,
    )
    planes_ext = with_halo(planes, h)
    t_above, t_below, t_left, t_right = plus_halo(tracer)
    mask_ext = planes_ext[0]
    m_above = mask_ext[None, h - 1 : h, h:-h]
    m_below = mask_ext[None, h + ocean_rows : h + ocean_rows + 1, h:-h]
    m_left = mask_ext[None, h:-h, h - 1 : h]
    m_right = mask_ext[None, h:-h, h + ocean_cols : h + ocean_cols + 1]
    tracer_mixed = diffuse(
        tracer, t_above, t_below, t_left, t_right, mask[None], m_above, m_below, m_left, m_right
    )

    owners = group_owner[:, 0]
    slots = owners * capacity + column_ranks(owners, peers)
    initial = atm_state.astype(jnp.bfloat16)
    outgoing = place_columns(initial, slots, total_slots)
    arrived = lax.all_to_all(outgoing, ("wide", "narrow"), split_axis=0, concat_axis=0, tiled=True)
    physics_out, tracer_mixed, planes_ext = lax.optimization_barrier(
        (physics(regime_ops[0], arrived, flux_map), tracer_mixed, planes_ext)
    )
    back = lax.all_to_all(
        physics_out,
        ("wide", "narrow"),
        split_axis=0,
        concat_axis=0,
        tiled=True,
    )
    returned = jnp.take(back, slots, axis=0, mode="clip")
    atm_new, flux_cols = unpack(returned, atm_state)
    mask_ext = planes_ext[0]
    eta = planes_ext[1]
    flow_u = planes_ext[2]
    flow_v = planes_ext[3]
    src_ext = planes_ext[4 : 4 + kk].astype(jnp.int32)
    weight_ext = planes_ext[4 + kk : 4 + 2 * kk]

    flux_block = flux_cols.astype(jnp.bfloat16).reshape(nflux, block_rows, AC)
    flux_ext = with_halo(flux_block, ATM_HALO)
    ocean_flux = remap(
        flux_ext,
        src_ext,
        weight_ext,
        ocean_rows,
        ocean_cols,
        wide_count * block_rows,
        narrow_count * AC,
    )

    inner = (slice(h, h + ocean_rows), slice(h, h + ocean_cols))
    tracer_new = tracer_mixed.at[0].add(heat_gain * mask * ocean_flux[0][inner])

    mask_east = next_col(mask_ext)
    mask_north = next_row(mask_ext)
    for _ in range(NSUB):
        flow_u = momentum(flow_u, eta, next_col(eta), mask_ext, mask_east, ocean_flux[2])
        flow_v = momentum(flow_v, eta, next_row(eta), mask_ext, mask_north, ocean_flux[3])
        eta = continuity(
            eta, flow_u, prev_col(flow_u), flow_v, prev_row(flow_v), mask_ext, ocean_flux[1]
        )
    return (atm_new, tracer_new, eta[inner], jnp.stack([flow_u[inner], flow_v[inner]]))


def solution(mesh):
    in_specs = (
        P(None, ("wide", "narrow")),
        P(("wide", "narrow"), None),
        P(("wide", "narrow"), None, None, None),
        P(),
        P(None, "wide", "narrow"),
        P(None, "wide", "narrow"),
        P("wide", "narrow"),
        P(None, "wide", "narrow"),
        P("wide", "narrow"),
        P(None, "wide", "narrow"),
    )
    out_specs = (
        P(None, ("wide", "narrow")),
        P(None, "wide", "narrow"),
        P("wide", "narrow"),
        P(None, "wide", "narrow"),
    )

    return jax.shard_map(per_device, mesh=mesh, in_specs=in_specs, out_specs=out_specs, check_vma=False)
```

```python
import jax
import jax.numpy as jnp
from jax import lax
from jax.sharding import PartitionSpec as P
from jax.experimental import pallas as pl

AC = 128
NSUB = 4
OCEAN_HALO = NSUB
ATM_HALO = OCEAN_HALO // 2 + 1


relax_rate = 0.5
kappa_mix = 0.2
heat_gain = 0.5
gravity = 0.7
depth_mean = 0.7
wind_gain = 0.3
fresh_gain = 0.3


def shift_pairs(count, step):
    return [(i, i + step) for i in range(count) if 0 <= i + step < count]


def with_halo(cells, width):
    wide_count = lax.axis_size("wide")
    narrow_count = lax.axis_size("narrow")
    rows = cells.shape[-2]
    cols = cells.shape[-1]
    above = lax.ppermute(cells[..., rows - width :, :], "wide", shift_pairs(wide_count, 1))
    below = lax.ppermute(cells[..., :width, :], "wide", shift_pairs(wide_count, -1))
    cells = jnp.concatenate([above, cells, below], axis=-2)
    left = lax.ppermute(cells[..., cols - width :], "narrow", shift_pairs(narrow_count, 1))
    right = lax.ppermute(cells[..., :width], "narrow", shift_pairs(narrow_count, -1))
    return jnp.concatenate([left, cells, right], axis=-1)


def plus_halo(cells):
    wide_count = lax.axis_size("wide")
    narrow_count = lax.axis_size("narrow")
    rows = cells.shape[-2]
    cols = cells.shape[-1]
    above = lax.ppermute(cells[:, rows - 1 :, :], "wide", shift_pairs(wide_count, 1))
    below = lax.ppermute(cells[:, :1, :], "wide", shift_pairs(wide_count, -1))
    left = lax.ppermute(cells[:, :, cols - 1], "narrow", shift_pairs(narrow_count, 1))
    right = lax.ppermute(cells[:, :, 0], "narrow", shift_pairs(narrow_count, -1))
    return above, below, left[:, :, None], right[:, :, None]


def column_ranks(owners, peers):
    onehot = (owners[:, None] == jnp.arange(peers, dtype=jnp.int32)[None, :]).astype(jnp.int32)
    before = jnp.cumsum(onehot, axis=0) - onehot
    return jnp.sum(before * onehot, axis=1)


def block_width():
    return 512


def place_columns(source, slots, total):
    width = block_width()
    pieces = []
    for start in range(0, total, width):
        selector = ((start + jnp.arange(width, dtype=jnp.int32))[:, None] == slots[None, :]).astype(
            jnp.bfloat16
        )
        pieces.append(
            lax.dot_general(
                selector, source, (((1,), (1,)), ((), ())), preferred_element_type=jnp.float32
            ).astype(jnp.bfloat16)
        )
    return jnp.concatenate(pieces, axis=0)


def physics_kernel(x_ref, op_ref, fm_ref, out_ref):
    features = x_ref.shape[1]
    initial = x_ref[...].astype(jnp.float32)
    current = initial
    for sweep in range(op_ref.shape[0]):
        mixed = jnp.dot(
            current.astype(jnp.bfloat16), op_ref[sweep], preferred_element_type=jnp.float32
        )
        current = current + relax_rate * jnp.tanh(mixed)
    final = current.astype(jnp.bfloat16)
    out_ref[:, :features] = (current - initial).astype(jnp.bfloat16)
    out_ref[:, features:] = jnp.dot(
        final, fm_ref[...], preferred_element_type=jnp.float32
    ).astype(jnp.bfloat16)


def physics(operators, columns, flux_map):
    slots, features = columns.shape
    nflux = flux_map.shape[1]
    tile = min(slots, 2048)
    sweeps = operators.shape[0]
    return pl.pallas_call(
        physics_kernel,
        out_shape=jax.ShapeDtypeStruct((slots, features + nflux), jnp.bfloat16),
        grid=(slots // tile,),
        in_specs=[
            pl.BlockSpec((tile, features), lambda i: (i, 0)),
            pl.BlockSpec((sweeps, features, features), lambda i: (0, 0, 0)),
            pl.BlockSpec((features, nflux), lambda i: (0, 0)),
        ],
        out_specs=pl.BlockSpec((tile, features + nflux), lambda i: (i, 0)),
        cost_estimate=pl.CostEstimate(
            flops=2 * slots * features * (sweeps * features + nflux),
            transcendentals=sweeps * slots * features,
            bytes_accessed=2 * slots * (2 * features + nflux) + 2 * sweeps * features * features,
        ),
    )(columns, operators, flux_map)


def unpack_kernel(got_ref, atm_ref, eye_ref, atm_out_ref, flux_out_ref):
    features = atm_ref.shape[0]
    turned = lax.dot_general(
        eye_ref[...], got_ref[...], (((1,), (1,)), ((), ())), preferred_element_type=jnp.float32
    )
    atm_out_ref[...] = atm_ref[...] + turned[:features]
    flux_out_ref[...] = turned[features:].astype(flux_out_ref.dtype)


def unpack(got, atm_state):
    columns, width = got.shape
    features = atm_state.shape[0]
    tile = min(columns, 512)
    eye = jnp.eye(width, dtype=jnp.bfloat16)
    return pl.pallas_call(
        unpack_kernel,
        out_shape=(
            jax.ShapeDtypeStruct((features, columns), jnp.float32),
            jax.ShapeDtypeStruct((width - features, columns), jnp.bfloat16),
        ),
        grid=(columns // tile,),
        in_specs=[
            pl.BlockSpec((tile, width), lambda i: (i, 0)),
            pl.BlockSpec((features, tile), lambda i: (0, i)),
            pl.BlockSpec((width, width), lambda i: (0, 0)),
        ],
        out_specs=(
            pl.BlockSpec((features, tile), lambda i: (0, i)),
            pl.BlockSpec((width - features, tile), lambda i: (0, i)),
        ),
        cost_estimate=pl.CostEstimate(
            flops=2 * columns * width * width,
            transcendentals=0,
            bytes_accessed=2 * columns * width + 8 * columns * features + 2 * columns * width,
        ),
    )(got, atm_state, eye)


def selector(count, origin, offset, limit, base, size):
    fine = origin + jnp.arange(count, dtype=jnp.int32)
    coarse = jnp.clip(fine // 2 + offset, 0, limit - 1) - base
    return (coarse[:, None] == jnp.arange(size, dtype=jnp.int32)[None, :]).astype(jnp.bfloat16)


def remap(flux_ext, src_ext, weight_ext, ocean_rows, ocean_cols, atm_rows, atm_cols):
    nflux = flux_ext.shape[0]
    ext_r = src_ext.shape[1]
    ext_c = src_ext.shape[2]
    block_r = flux_ext.shape[1] - 2 * ATM_HALO
    block_c = flux_ext.shape[2] - 2 * ATM_HALO
    my_wide = lax.axis_index("wide")
    my_narrow = lax.axis_index("narrow")
    row0 = my_wide * ocean_rows - OCEAN_HALO
    col0 = my_narrow * ocean_cols - OCEAN_HALO
    arow0 = my_wide * block_r - ATM_HALO
    acol0 = my_narrow * block_c - ATM_HALO
    col_sel = jnp.concatenate(
        [
            selector(ext_c, col0, dc, atm_cols, acol0, flux_ext.shape[2]).T
            for dc in (-1, 0, 1)
        ],
        axis=1,
    )
    by_cols = jnp.dot(
        flux_ext.reshape(nflux * flux_ext.shape[1], flux_ext.shape[2]),
        col_sel,
        preferred_element_type=jnp.float32,
    ).astype(jnp.bfloat16)
    by_cols = by_cols.reshape(nflux, flux_ext.shape[1], 3 * ext_c)
    ocean_flux = jnp.zeros((nflux, ext_r, ext_c), jnp.float32)
    for dr in (-1, 0, 1):
        row_sel = selector(ext_r, row0, dr, atm_rows, arow0, flux_ext.shape[1])
        shifted = jnp.einsum(
            "ap,fpx->fax", row_sel, by_cols, preferred_element_type=jnp.float32
        )
        for dc in (-1, 0, 1):
            code = (dr + 1) * 3 + (dc + 1)
            weight_sum = jnp.sum(jnp.where(src_ext == code, weight_ext, 0.0), axis=0)
            window = shifted[:, :, (dc + 1) * ext_c : (dc + 2) * ext_c]
            ocean_flux = ocean_flux + weight_sum[None] * window
    return ocean_flux


def diffuse(centre, above, below, left, right, mask, m_above, m_below, m_left, m_right):
    north = jnp.concatenate([centre[:, 1:, :], below], axis=1)
    south = jnp.concatenate([above, centre[:, :-1, :]], axis=1)
    east = jnp.concatenate([centre[:, :, 1:], right], axis=2)
    west = jnp.concatenate([left, centre[:, :, :-1]], axis=2)
    mn = jnp.concatenate([mask[:, 1:, :], m_below], axis=1)
    ms = jnp.concatenate([m_above, mask[:, :-1, :]], axis=1)
    me = jnp.concatenate([mask[:, :, 1:], m_right], axis=2)
    mw = jnp.concatenate([m_left, mask[:, :, :-1]], axis=2)
    summed = jnp.zeros_like(centre)
    for nb, mb in ((north, mn), (south, ms), (east, me), (west, mw)):
        summed = summed + mask * mb * (nb - centre)
    return centre + kappa_mix * summed


def momentum(flow, height, height_next, mask, mask_next, stress):
    return mask * mask_next * (flow - gravity * (height_next - height) + wind_gain * stress)


def continuity(height, flow_u, flow_u_west, flow_v, flow_v_south, mask, fresh):
    return mask * (
        height - depth_mean * (flow_u - flow_u_west + (flow_v - flow_v_south)) + fresh_gain * fresh
    )


def next_col(x):
    return jnp.concatenate([x[:, 1:], jnp.zeros_like(x[:, :1])], axis=1)


def next_row(x):
    return jnp.concatenate([x[1:, :], jnp.zeros_like(x[:1, :])], axis=0)


def prev_col(x):
    return jnp.concatenate([jnp.zeros_like(x[:, :1]), x[:, :-1]], axis=1)


def prev_row(x):
    return jnp.concatenate([jnp.zeros_like(x[:1, :]), x[:-1, :]], axis=0)


def per_device(
    atm_state,
    group_owner,
    regime_ops,
    flux_map,
    remap_src,
    remap_weight,
    ocean_mask,
    tracer,
    surface_height,
    transports,
):
    peers = lax.axis_size(("wide", "narrow"))
    wide_count = lax.axis_size("wide")
    narrow_count = lax.axis_size("narrow")
    columns_here = atm_state.shape[1]
    nflux = flux_map.shape[1]
    capacity = 2 * columns_here // peers
    total_slots = peers * capacity
    block_rows = columns_here // AC
    ocean_rows = remap_src.shape[1]
    ocean_cols = remap_src.shape[2]
    kk = remap_src.shape[0]
    h = OCEAN_HALO

    mask = ocean_mask.astype(jnp.float32)
    planes = jnp.concatenate(
        [
            mask[None],
            surface_height[None],
            transports,
            remap_src.astype(jnp.float32),
            remap_weight,
        ],
        axis=0,
    )
    planes_ext = with_halo(planes, h)
    t_above, t_below, t_left, t_right = plus_halo(tracer)
    mask_ext = planes_ext[0]
    m_above = mask_ext[None, h - 1 : h, h:-h]
    m_below = mask_ext[None, h + ocean_rows : h + ocean_rows + 1, h:-h]
    m_left = mask_ext[None, h:-h, h - 1 : h]
    m_right = mask_ext[None, h:-h, h + ocean_cols : h + ocean_cols + 1]
    tracer_mixed = diffuse(
        tracer, t_above, t_below, t_left, t_right, mask[None], m_above, m_below, m_left, m_right
    )

    owners = group_owner[:, 0]
    slots = owners * capacity + column_ranks(owners, peers)
    initial = atm_state.astype(jnp.bfloat16)
    outgoing = place_columns(initial, slots, total_slots)
    arrived = lax.all_to_all(outgoing, ("wide", "narrow"), split_axis=0, concat_axis=0, tiled=True)
    back = lax.all_to_all(
        physics(regime_ops[0], arrived, flux_map),
        ("wide", "narrow"),
        split_axis=0,
        concat_axis=0,
        tiled=True,
    )
    returned = jnp.take(back, slots, axis=0, mode="clip")
    atm_new, flux_cols = unpack(returned, atm_state)
    mask_ext = planes_ext[0]
    eta = planes_ext[1]
    flow_u = planes_ext[2]
    flow_v = planes_ext[3]
    src_ext = planes_ext[4 : 4 + kk].astype(jnp.int32)
    weight_ext = planes_ext[4 + kk : 4 + 2 * kk]

    flux_block = flux_cols.astype(jnp.bfloat16).reshape(nflux, block_rows, AC)
    flux_ext = with_halo(flux_block, ATM_HALO)
    ocean_flux = remap(
        flux_ext,
        src_ext,
        weight_ext,
        ocean_rows,
        ocean_cols,
        wide_count * block_rows,
        narrow_count * AC,
    )

    inner = (slice(h, h + ocean_rows), slice(h, h + ocean_cols))
    tracer_new = tracer_mixed.at[0].add(heat_gain * mask * ocean_flux[0][inner])

    mask_east = next_col(mask_ext)
    mask_north = next_row(mask_ext)
    for _ in range(NSUB):
        flow_u = momentum(flow_u, eta, next_col(eta), mask_ext, mask_east, ocean_flux[2])
        flow_v = momentum(flow_v, eta, next_row(eta), mask_ext, mask_north, ocean_flux[3])
        eta = continuity(
            eta, flow_u, prev_col(flow_u), flow_v, prev_row(flow_v), mask_ext, ocean_flux[1]
        )
    return (atm_new, tracer_new, eta[inner], jnp.stack([flow_u[inner], flow_v[inner]]))


def solution(mesh):
    in_specs = (
        P(None, ("wide", "narrow")),
        P(("wide", "narrow"), None),
        P(("wide", "narrow"), None, None, None),
        P(),
        P(None, "wide", "narrow"),
        P(None, "wide", "narrow"),
        P("wide", "narrow"),
        P(None, "wide", "narrow"),
        P("wide", "narrow"),
        P(None, "wide", "narrow"),
    )
    out_specs = (
        P(None, ("wide", "narrow")),
        P(None, "wide", "narrow"),
        P("wide", "narrow"),
        P(None, "wide", "narrow"),
    )

    return jax.shard_map(per_device, mesh=mesh, in_specs=in_specs, out_specs=out_specs, check_vma=False)
```

```python
import jax
import jax.numpy as jnp
from jax import lax
from jax.sharding import PartitionSpec as P
from jax.experimental import pallas as pl

AC = 128
NSUB = 4
OCEAN_HALO = NSUB
ATM_HALO = OCEAN_HALO // 2 + 1


relax_rate = 0.5
kappa_mix = 0.2
heat_gain = 0.5
gravity = 0.7
depth_mean = 0.7
wind_gain = 0.3
fresh_gain = 0.3


def shift_pairs(count, step):
    return [(i, i + step) for i in range(count) if 0 <= i + step < count]


def with_halo(cells, width):
    wide_count = lax.axis_size("wide")
    narrow_count = lax.axis_size("narrow")
    rows = cells.shape[-2]
    cols = cells.shape[-1]
    above = lax.ppermute(cells[..., rows - width :, :], "wide", shift_pairs(wide_count, 1))
    below = lax.ppermute(cells[..., :width, :], "wide", shift_pairs(wide_count, -1))
    cells = jnp.concatenate([above, cells, below], axis=-2)
    left = lax.ppermute(cells[..., cols - width :], "narrow", shift_pairs(narrow_count, 1))
    right = lax.ppermute(cells[..., :width], "narrow", shift_pairs(narrow_count, -1))
    return jnp.concatenate([left, cells, right], axis=-1)


def plus_halo(cells):
    wide_count = lax.axis_size("wide")
    narrow_count = lax.axis_size("narrow")
    rows = cells.shape[-2]
    cols = cells.shape[-1]
    above = lax.ppermute(cells[:, rows - 1 :, :], "wide", shift_pairs(wide_count, 1))
    below = lax.ppermute(cells[:, :1, :], "wide", shift_pairs(wide_count, -1))
    left = lax.ppermute(cells[:, :, cols - 1], "narrow", shift_pairs(narrow_count, 1))
    right = lax.ppermute(cells[:, :, 0], "narrow", shift_pairs(narrow_count, -1))
    return above, below, left[:, :, None], right[:, :, None]


def column_ranks(owners, peers):
    onehot = (owners[:, None] == jnp.arange(peers, dtype=jnp.int32)[None, :]).astype(jnp.int32)
    before = jnp.cumsum(onehot, axis=0) - onehot
    return jnp.sum(before * onehot, axis=1)


def block_width():
    return 512


def place_columns(source, slots, total):
    width = block_width()
    pieces = []
    for start in range(0, total, width):
        selector = ((start + jnp.arange(width, dtype=jnp.int32))[:, None] == slots[None, :]).astype(
            jnp.bfloat16
        )
        pieces.append(
            lax.dot_general(
                selector, source, (((1,), (1,)), ((), ())), preferred_element_type=jnp.float32
            ).astype(jnp.bfloat16)
        )
    return jnp.concatenate(pieces, axis=0)


def physics_kernel(x_ref, op_ref, fm_ref, out_ref):
    features = x_ref.shape[1]
    initial = x_ref[...].astype(jnp.float32)
    current = initial
    for sweep in range(op_ref.shape[0]):
        mixed = jnp.dot(
            current.astype(jnp.bfloat16), op_ref[sweep], preferred_element_type=jnp.float32
        )
        current = current + relax_rate * jnp.tanh(mixed)
    final = current.astype(jnp.bfloat16)
    out_ref[:, :features] = (current - initial).astype(jnp.bfloat16)
    out_ref[:, features:] = jnp.dot(
        final, fm_ref[...], preferred_element_type=jnp.float32
    ).astype(jnp.bfloat16)


def physics(operators, columns, flux_map):
    slots, features = columns.shape
    nflux = flux_map.shape[1]
    tile = min(slots, 2048)
    sweeps = operators.shape[0]
    return pl.pallas_call(
        physics_kernel,
        out_shape=jax.ShapeDtypeStruct((slots, features + nflux), jnp.bfloat16),
        grid=(slots // tile,),
        in_specs=[
            pl.BlockSpec((tile, features), lambda i: (i, 0)),
            pl.BlockSpec((sweeps, features, features), lambda i: (0, 0, 0)),
            pl.BlockSpec((features, nflux), lambda i: (0, 0)),
        ],
        out_specs=pl.BlockSpec((tile, features + nflux), lambda i: (i, 0)),
        cost_estimate=pl.CostEstimate(
            flops=2 * slots * features * (sweeps * features + nflux),
            transcendentals=sweeps * slots * features,
            bytes_accessed=2 * slots * (2 * features + nflux) + 2 * sweeps * features * features,
        ),
    )(columns, operators, flux_map)


def unpack_kernel(got_ref, atm_ref, eye_ref, atm_out_ref, flux_out_ref):
    features = atm_ref.shape[0]
    turned = lax.dot_general(
        eye_ref[...], got_ref[...], (((1,), (1,)), ((), ())), preferred_element_type=jnp.float32
    )
    atm_out_ref[...] = atm_ref[...] + turned[:features]
    flux_out_ref[...] = turned[features:].astype(flux_out_ref.dtype)


def unpack(got, atm_state):
    columns, width = got.shape
    features = atm_state.shape[0]
    tile = min(columns, 512)
    eye = jnp.eye(width, dtype=jnp.bfloat16)
    return pl.pallas_call(
        unpack_kernel,
        out_shape=(
            jax.ShapeDtypeStruct((features, columns), jnp.float32),
            jax.ShapeDtypeStruct((width - features, columns), jnp.bfloat16),
        ),
        grid=(columns // tile,),
        in_specs=[
            pl.BlockSpec((tile, width), lambda i: (i, 0)),
            pl.BlockSpec((features, tile), lambda i: (0, i)),
            pl.BlockSpec((width, width), lambda i: (0, 0)),
        ],
        out_specs=(
            pl.BlockSpec((features, tile), lambda i: (0, i)),
            pl.BlockSpec((width - features, tile), lambda i: (0, i)),
        ),
        cost_estimate=pl.CostEstimate(
            flops=2 * columns * width * width,
            transcendentals=0,
            bytes_accessed=2 * columns * width + 8 * columns * features + 2 * columns * width,
        ),
    )(got, atm_state, eye)


def selector(count, origin, offset, limit, base, size):
    fine = origin + jnp.arange(count, dtype=jnp.int32)
    coarse = jnp.clip(fine // 2 + offset, 0, limit - 1) - base
    return (coarse[:, None] == jnp.arange(size, dtype=jnp.int32)[None, :]).astype(jnp.bfloat16)


def remap(flux_ext, src_ext, weight_ext, ocean_rows, ocean_cols, atm_rows, atm_cols):
    nflux = flux_ext.shape[0]
    ext_r = src_ext.shape[1]
    ext_c = src_ext.shape[2]
    block_r = flux_ext.shape[1] - 2 * ATM_HALO
    block_c = flux_ext.shape[2] - 2 * ATM_HALO
    my_wide = lax.axis_index("wide")
    my_narrow = lax.axis_index("narrow")
    row0 = my_wide * ocean_rows - OCEAN_HALO
    col0 = my_narrow * ocean_cols - OCEAN_HALO
    arow0 = my_wide * block_r - ATM_HALO
    acol0 = my_narrow * block_c - ATM_HALO
    col_sel = jnp.concatenate(
        [
            selector(ext_c, col0, dc, atm_cols, acol0, flux_ext.shape[2]).T
            for dc in (-1, 0, 1)
        ],
        axis=1,
    )
    by_cols = jnp.einsum(
        "fpt,tx->fpx", flux_ext, col_sel, preferred_element_type=jnp.float32
    ).astype(jnp.bfloat16)
    ocean_flux = jnp.zeros((nflux, ext_r, ext_c), jnp.float32)
    for dr in (-1, 0, 1):
        row_sel = selector(ext_r, row0, dr, atm_rows, arow0, flux_ext.shape[1])
        shifted = jnp.einsum(
            "ap,fpx->fax", row_sel, by_cols, preferred_element_type=jnp.float32
        )
        for dc in (-1, 0, 1):
            code = (dr + 1) * 3 + (dc + 1)
            weight_sum = jnp.sum(jnp.where(src_ext == code, weight_ext, 0.0), axis=0)
            window = shifted[:, :, (dc + 1) * ext_c : (dc + 2) * ext_c]
            ocean_flux = ocean_flux + weight_sum[None] * window
    return ocean_flux


def diffuse(centre, above, below, left, right, mask, m_above, m_below, m_left, m_right):
    north = jnp.concatenate([centre[:, 1:, :], below], axis=1)
    south = jnp.concatenate([above, centre[:, :-1, :]], axis=1)
    east = jnp.concatenate([centre[:, :, 1:], right], axis=2)
    west = jnp.concatenate([left, centre[:, :, :-1]], axis=2)
    mn = jnp.concatenate([mask[:, 1:, :], m_below], axis=1)
    ms = jnp.concatenate([m_above, mask[:, :-1, :]], axis=1)
    me = jnp.concatenate([mask[:, :, 1:], m_right], axis=2)
    mw = jnp.concatenate([m_left, mask[:, :, :-1]], axis=2)
    summed = jnp.zeros_like(centre)
    for nb, mb in ((north, mn), (south, ms), (east, me), (west, mw)):
        summed = summed + mask * mb * (nb - centre)
    return centre + kappa_mix * summed


def momentum(flow, height, height_next, mask, mask_next, stress):
    return mask * mask_next * (flow - gravity * (height_next - height) + wind_gain * stress)


def continuity(height, flow_u, flow_u_west, flow_v, flow_v_south, mask, fresh):
    return mask * (
        height - depth_mean * (flow_u - flow_u_west + (flow_v - flow_v_south)) + fresh_gain * fresh
    )


def next_col(x):
    return jnp.concatenate([x[:, 1:], jnp.zeros_like(x[:, :1])], axis=1)


def next_row(x):
    return jnp.concatenate([x[1:, :], jnp.zeros_like(x[:1, :])], axis=0)


def prev_col(x):
    return jnp.concatenate([jnp.zeros_like(x[:, :1]), x[:, :-1]], axis=1)


def prev_row(x):
    return jnp.concatenate([jnp.zeros_like(x[:1, :]), x[:-1, :]], axis=0)


def per_device(
    atm_state,
    group_owner,
    regime_ops,
    flux_map,
    remap_src,
    remap_weight,
    ocean_mask,
    tracer,
    surface_height,
    transports,
):
    peers = lax.axis_size(("wide", "narrow"))
    wide_count = lax.axis_size("wide")
    narrow_count = lax.axis_size("narrow")
    columns_here = atm_state.shape[1]
    nflux = flux_map.shape[1]
    capacity = 2 * columns_here // peers
    total_slots = peers * capacity
    block_rows = columns_here // AC
    ocean_rows = remap_src.shape[1]
    ocean_cols = remap_src.shape[2]
    kk = remap_src.shape[0]
    h = OCEAN_HALO

    mask = ocean_mask.astype(jnp.float32)
    planes = jnp.concatenate(
        [mask[None], surface_height[None], transports, remap_src.astype(jnp.float32), remap_weight],
        axis=0,
    )
    planes_ext = with_halo(planes, h)
    t_above, t_below, t_left, t_right = plus_halo(tracer)
    mask_ext = planes_ext[0]
    m_above = mask_ext[None, h - 1 : h, h:-h]
    m_below = mask_ext[None, h + ocean_rows : h + ocean_rows + 1, h:-h]
    m_left = mask_ext[None, h:-h, h - 1 : h]
    m_right = mask_ext[None, h:-h, h + ocean_cols : h + ocean_cols + 1]
    tracer_mixed = diffuse(
        tracer, t_above, t_below, t_left, t_right, mask[None], m_above, m_below, m_left, m_right
    )

    owners = group_owner[:, 0]
    slots = owners * capacity + column_ranks(owners, peers)
    initial = atm_state.astype(jnp.bfloat16)
    outgoing = place_columns(initial, slots, total_slots)
    arrived = lax.all_to_all(outgoing, ("wide", "narrow"), split_axis=0, concat_axis=0, tiled=True)
    back = lax.all_to_all(
        physics(regime_ops[0], arrived, flux_map),
        ("wide", "narrow"),
        split_axis=0,
        concat_axis=0,
        tiled=True,
    )
    returned = jnp.take(back, slots, axis=0, mode="clip")
    atm_new, flux_cols = unpack(returned, atm_state)
    mask_ext = planes_ext[0]
    eta = planes_ext[1]
    flow_u = planes_ext[2]
    flow_v = planes_ext[3]
    src_ext = planes_ext[4 : 4 + kk].astype(jnp.int32)
    weight_ext = planes_ext[4 + kk : 4 + 2 * kk]

    flux_block = flux_cols.astype(jnp.bfloat16).reshape(nflux, block_rows, AC)
    flux_ext = with_halo(flux_block, ATM_HALO)
    ocean_flux = remap(
        flux_ext,
        src_ext,
        weight_ext,
        ocean_rows,
        ocean_cols,
        wide_count * block_rows,
        narrow_count * AC,
    )

    inner = (slice(h, h + ocean_rows), slice(h, h + ocean_cols))
    tracer_new = tracer_mixed.at[0].add(heat_gain * mask * ocean_flux[0][inner])

    mask_east = next_col(mask_ext)
    mask_north = next_row(mask_ext)
    for _ in range(NSUB):
        flow_u = momentum(flow_u, eta, next_col(eta), mask_ext, mask_east, ocean_flux[2])
        flow_v = momentum(flow_v, eta, next_row(eta), mask_ext, mask_north, ocean_flux[3])
        eta = continuity(
            eta, flow_u, prev_col(flow_u), flow_v, prev_row(flow_v), mask_ext, ocean_flux[1]
        )
    return (atm_new, tracer_new, eta[inner], jnp.stack([flow_u[inner], flow_v[inner]]))


def solution(mesh):
    in_specs = (
        P(None, ("wide", "narrow")),
        P(("wide", "narrow"), None),
        P(("wide", "narrow"), None, None, None),
        P(),
        P(None, "wide", "narrow"),
        P(None, "wide", "narrow"),
        P("wide", "narrow"),
        P(None, "wide", "narrow"),
        P("wide", "narrow"),
        P(None, "wide", "narrow"),
    )
    out_specs = (
        P(None, ("wide", "narrow")),
        P(None, "wide", "narrow"),
        P("wide", "narrow"),
        P(None, "wide", "narrow"),
    )

    return jax.shard_map(per_device, mesh=mesh, in_specs=in_specs, out_specs=out_specs, check_vma=False)
```

```python
import jax
import jax.numpy as jnp
from jax import lax
from jax.sharding import PartitionSpec as P
from jax.experimental import pallas as pl

AC = 128
NSUB = 4
OCEAN_HALO = NSUB
ATM_HALO = OCEAN_HALO // 2 + 1


relax_rate = 0.5
kappa_mix = 0.2
heat_gain = 0.5
gravity = 0.7
depth_mean = 0.7
wind_gain = 0.3
fresh_gain = 0.3


def shift_pairs(count, step):
    return [(i, i + step) for i in range(count) if 0 <= i + step < count]


def with_halo(cells, width):
    wide_count = lax.axis_size("wide")
    narrow_count = lax.axis_size("narrow")
    rows = cells.shape[-2]
    cols = cells.shape[-1]
    above = lax.ppermute(cells[..., rows - width :, :], "wide", shift_pairs(wide_count, 1))
    below = lax.ppermute(cells[..., :width, :], "wide", shift_pairs(wide_count, -1))
    cells = jnp.concatenate([above, cells, below], axis=-2)
    left = lax.ppermute(cells[..., cols - width :], "narrow", shift_pairs(narrow_count, 1))
    right = lax.ppermute(cells[..., :width], "narrow", shift_pairs(narrow_count, -1))
    return jnp.concatenate([left, cells, right], axis=-1)


def plus_halo(cells):
    wide_count = lax.axis_size("wide")
    narrow_count = lax.axis_size("narrow")
    rows = cells.shape[-2]
    cols = cells.shape[-1]
    above = lax.ppermute(cells[:, rows - 1 :, :], "wide", shift_pairs(wide_count, 1))
    below = lax.ppermute(cells[:, :1, :], "wide", shift_pairs(wide_count, -1))
    left = lax.ppermute(cells[:, :, cols - 1], "narrow", shift_pairs(narrow_count, 1))
    right = lax.ppermute(cells[:, :, 0], "narrow", shift_pairs(narrow_count, -1))
    return above, below, left[:, :, None], right[:, :, None]


def column_ranks(owners, peers):
    onehot = (owners[:, None] == jnp.arange(peers, dtype=jnp.int32)[None, :]).astype(jnp.int32)
    before = jnp.cumsum(onehot, axis=0) - onehot
    return jnp.sum(before * onehot, axis=1)


def block_width():
    return 512


def place_columns(source, slots, total):
    width = block_width()
    pieces = []
    for start in range(0, total, width):
        selector = ((start + jnp.arange(width, dtype=jnp.int32))[:, None] == slots[None, :]).astype(
            jnp.bfloat16
        )
        pieces.append(
            lax.dot_general(
                selector, source, (((1,), (1,)), ((), ())), preferred_element_type=jnp.float32
            ).astype(jnp.bfloat16)
        )
    return jnp.concatenate(pieces, axis=0)


def physics_kernel(x_ref, op_ref, fm_ref, out_ref):
    features = x_ref.shape[1]
    initial = x_ref[...].astype(jnp.float32)
    current = initial
    for sweep in range(op_ref.shape[0]):
        mixed = jnp.dot(
            current.astype(jnp.bfloat16), op_ref[sweep], preferred_element_type=jnp.float32
        )
        current = current + relax_rate * jnp.tanh(mixed)
    final = current.astype(jnp.bfloat16)
    out_ref[:, :features] = (current - initial).astype(jnp.bfloat16)
    out_ref[:, features:] = jnp.dot(
        final, fm_ref[...], preferred_element_type=jnp.float32
    ).astype(jnp.bfloat16)


def physics(operators, columns, flux_map):
    slots, features = columns.shape
    nflux = flux_map.shape[1]
    tile = min(slots, 2048)
    sweeps = operators.shape[0]
    return pl.pallas_call(
        physics_kernel,
        out_shape=jax.ShapeDtypeStruct((slots, features + nflux), jnp.bfloat16),
        grid=(slots // tile,),
        in_specs=[
            pl.BlockSpec((tile, features), lambda i: (i, 0)),
            pl.BlockSpec((sweeps, features, features), lambda i: (0, 0, 0)),
            pl.BlockSpec((features, nflux), lambda i: (0, 0)),
        ],
        out_specs=pl.BlockSpec((tile, features + nflux), lambda i: (i, 0)),
        cost_estimate=pl.CostEstimate(
            flops=2 * slots * features * (sweeps * features + nflux),
            transcendentals=sweeps * slots * features,
            bytes_accessed=2 * slots * (2 * features + nflux) + 2 * sweeps * features * features,
        ),
    )(columns, operators, flux_map)


def fetch_kernel(slots_ref, back_ref, atm_ref, atm_out_ref, flux_out_ref):
    features = atm_ref.shape[0]
    count = back_ref.shape[0]
    tile = slots_ref.shape[1]
    picked = (lax.broadcasted_iota(jnp.int32, (count, tile), 0) == slots_ref[...]).astype(
        jnp.bfloat16
    )
    got = lax.dot_general(
        back_ref[...], picked, (((0,), (0,)), ((), ())), preferred_element_type=jnp.float32
    )
    atm_out_ref[...] = atm_ref[...] + got[:features]
    flux_out_ref[...] = got[features:].astype(flux_out_ref.dtype)


def fetch(back, slots, atm_state):
    count, width = back.shape
    features, columns = atm_state.shape
    tile = min(columns, 256)
    return pl.pallas_call(
        fetch_kernel,
        out_shape=(
            jax.ShapeDtypeStruct((features, columns), jnp.float32),
            jax.ShapeDtypeStruct((width - features, columns), jnp.bfloat16),
        ),
        grid=(columns // tile,),
        in_specs=[
            pl.BlockSpec((1, tile), lambda i: (0, i)),
            pl.BlockSpec((count, width), lambda i: (0, 0)),
            pl.BlockSpec((features, tile), lambda i: (0, i)),
        ],
        out_specs=(
            pl.BlockSpec((features, tile), lambda i: (0, i)),
            pl.BlockSpec((width - features, tile), lambda i: (0, i)),
        ),
        cost_estimate=pl.CostEstimate(
            flops=2 * count * width * columns,
            transcendentals=0,
            bytes_accessed=2 * count * width + 8 * columns * features + 2 * columns * width,
        ),
    )(slots.reshape(1, columns), back, atm_state)


def selector(count, origin, offset, limit, base, size):
    fine = origin + jnp.arange(count, dtype=jnp.int32)
    coarse = jnp.clip(fine // 2 + offset, 0, limit - 1) - base
    return (coarse[:, None] == jnp.arange(size, dtype=jnp.int32)[None, :]).astype(jnp.bfloat16)


def remap(flux_ext, src_ext, weight_ext, ocean_rows, ocean_cols, atm_rows, atm_cols):
    nflux = flux_ext.shape[0]
    ext_r = src_ext.shape[1]
    ext_c = src_ext.shape[2]
    block_r = flux_ext.shape[1] - 2 * ATM_HALO
    block_c = flux_ext.shape[2] - 2 * ATM_HALO
    my_wide = lax.axis_index("wide")
    my_narrow = lax.axis_index("narrow")
    row0 = my_wide * ocean_rows - OCEAN_HALO
    col0 = my_narrow * ocean_cols - OCEAN_HALO
    arow0 = my_wide * block_r - ATM_HALO
    acol0 = my_narrow * block_c - ATM_HALO
    col_sel = jnp.concatenate(
        [
            selector(ext_c, col0, dc, atm_cols, acol0, flux_ext.shape[2]).T
            for dc in (-1, 0, 1)
        ],
        axis=1,
    )
    by_cols = jnp.einsum(
        "fpt,tx->fpx", flux_ext, col_sel, preferred_element_type=jnp.float32
    ).astype(jnp.bfloat16)
    ocean_flux = jnp.zeros((nflux, ext_r, ext_c), jnp.float32)
    for dr in (-1, 0, 1):
        row_sel = selector(ext_r, row0, dr, atm_rows, arow0, flux_ext.shape[1])
        shifted = jnp.einsum(
            "ap,fpx->fax", row_sel, by_cols, preferred_element_type=jnp.float32
        )
        for dc in (-1, 0, 1):
            code = (dr + 1) * 3 + (dc + 1)
            weight_sum = jnp.sum(jnp.where(src_ext == code, weight_ext, 0.0), axis=0)
            window = shifted[:, :, (dc + 1) * ext_c : (dc + 2) * ext_c]
            ocean_flux = ocean_flux + weight_sum[None] * window
    return ocean_flux


def diffuse(centre, above, below, left, right, mask, m_above, m_below, m_left, m_right):
    north = jnp.concatenate([centre[:, 1:, :], below], axis=1)
    south = jnp.concatenate([above, centre[:, :-1, :]], axis=1)
    east = jnp.concatenate([centre[:, :, 1:], right], axis=2)
    west = jnp.concatenate([left, centre[:, :, :-1]], axis=2)
    mn = jnp.concatenate([mask[:, 1:, :], m_below], axis=1)
    ms = jnp.concatenate([m_above, mask[:, :-1, :]], axis=1)
    me = jnp.concatenate([mask[:, :, 1:], m_right], axis=2)
    mw = jnp.concatenate([m_left, mask[:, :, :-1]], axis=2)
    summed = jnp.zeros_like(centre)
    for nb, mb in ((north, mn), (south, ms), (east, me), (west, mw)):
        summed = summed + mask * mb * (nb - centre)
    return centre + kappa_mix * summed


def momentum(flow, height, height_next, mask, mask_next, stress):
    return mask * mask_next * (flow - gravity * (height_next - height) + wind_gain * stress)


def continuity(height, flow_u, flow_u_west, flow_v, flow_v_south, mask, fresh):
    return mask * (
        height - depth_mean * (flow_u - flow_u_west + (flow_v - flow_v_south)) + fresh_gain * fresh
    )


def next_col(x):
    return jnp.concatenate([x[:, 1:], jnp.zeros_like(x[:, :1])], axis=1)


def next_row(x):
    return jnp.concatenate([x[1:, :], jnp.zeros_like(x[:1, :])], axis=0)


def prev_col(x):
    return jnp.concatenate([jnp.zeros_like(x[:, :1]), x[:, :-1]], axis=1)


def prev_row(x):
    return jnp.concatenate([jnp.zeros_like(x[:1, :]), x[:-1, :]], axis=0)


def per_device(
    atm_state,
    group_owner,
    regime_ops,
    flux_map,
    remap_src,
    remap_weight,
    ocean_mask,
    tracer,
    surface_height,
    transports,
):
    peers = lax.axis_size(("wide", "narrow"))
    wide_count = lax.axis_size("wide")
    narrow_count = lax.axis_size("narrow")
    columns_here = atm_state.shape[1]
    nflux = flux_map.shape[1]
    capacity = 2 * columns_here // peers
    total_slots = peers * capacity
    block_rows = columns_here // AC
    ocean_rows = remap_src.shape[1]
    ocean_cols = remap_src.shape[2]
    kk = remap_src.shape[0]
    h = OCEAN_HALO

    mask = ocean_mask.astype(jnp.float32)
    planes = jnp.concatenate(
        [mask[None], surface_height[None], transports, remap_src.astype(jnp.float32), remap_weight],
        axis=0,
    )
    planes_ext = with_halo(planes, h)
    t_above, t_below, t_left, t_right = plus_halo(tracer)
    mask_ext = planes_ext[0]
    m_above = mask_ext[None, h - 1 : h, h:-h]
    m_below = mask_ext[None, h + ocean_rows : h + ocean_rows + 1, h:-h]
    m_left = mask_ext[None, h:-h, h - 1 : h]
    m_right = mask_ext[None, h:-h, h + ocean_cols : h + ocean_cols + 1]
    tracer_mixed = diffuse(
        tracer, t_above, t_below, t_left, t_right, mask[None], m_above, m_below, m_left, m_right
    )

    owners = group_owner[:, 0]
    slots = owners * capacity + column_ranks(owners, peers)
    initial = atm_state.astype(jnp.bfloat16)
    outgoing = place_columns(initial, slots, total_slots)
    arrived = lax.all_to_all(outgoing, ("wide", "narrow"), split_axis=0, concat_axis=0, tiled=True)
    back = lax.all_to_all(
        physics(regime_ops[0], arrived, flux_map),
        ("wide", "narrow"),
        split_axis=0,
        concat_axis=0,
        tiled=True,
    )
    atm_new, flux_cols = fetch(back, slots, atm_state)
    mask_ext = planes_ext[0]
    eta = planes_ext[1]
    flow_u = planes_ext[2]
    flow_v = planes_ext[3]
    src_ext = planes_ext[4 : 4 + kk].astype(jnp.int32)
    weight_ext = planes_ext[4 + kk : 4 + 2 * kk]

    flux_block = flux_cols.astype(jnp.bfloat16).reshape(nflux, block_rows, AC)
    flux_ext = with_halo(flux_block, ATM_HALO)
    ocean_flux = remap(
        flux_ext,
        src_ext,
        weight_ext,
        ocean_rows,
        ocean_cols,
        wide_count * block_rows,
        narrow_count * AC,
    )

    inner = (slice(h, h + ocean_rows), slice(h, h + ocean_cols))
    tracer_new = tracer_mixed.at[0].add(heat_gain * mask * ocean_flux[0][inner])

    mask_east = next_col(mask_ext)
    mask_north = next_row(mask_ext)
    for _ in range(NSUB):
        flow_u = momentum(flow_u, eta, next_col(eta), mask_ext, mask_east, ocean_flux[2])
        flow_v = momentum(flow_v, eta, next_row(eta), mask_ext, mask_north, ocean_flux[3])
        eta = continuity(
            eta, flow_u, prev_col(flow_u), flow_v, prev_row(flow_v), mask_ext, ocean_flux[1]
        )
    return (atm_new, tracer_new, eta[inner], jnp.stack([flow_u[inner], flow_v[inner]]))


def solution(mesh):
    in_specs = (
        P(None, ("wide", "narrow")),
        P(("wide", "narrow"), None),
        P(("wide", "narrow"), None, None, None),
        P(),
        P(None, "wide", "narrow"),
        P(None, "wide", "narrow"),
        P("wide", "narrow"),
        P(None, "wide", "narrow"),
        P("wide", "narrow"),
        P(None, "wide", "narrow"),
    )
    out_specs = (
        P(None, ("wide", "narrow")),
        P(None, "wide", "narrow"),
        P("wide", "narrow"),
        P(None, "wide", "narrow"),
    )

    return jax.shard_map(per_device, mesh=mesh, in_specs=in_specs, out_specs=out_specs, check_vma=False)
```

```python
import jax
import jax.numpy as jnp
from jax import lax
from jax.sharding import PartitionSpec as P
from jax.experimental import pallas as pl

AC = 128
NSUB = 4
OCEAN_HALO = NSUB
ATM_HALO = OCEAN_HALO // 2 + 1


relax_rate = 0.5
kappa_mix = 0.2
heat_gain = 0.5
gravity = 0.7
depth_mean = 0.7
wind_gain = 0.3
fresh_gain = 0.3


def shift_pairs(count, step):
    return [(i, i + step) for i in range(count) if 0 <= i + step < count]


def with_halo(cells, width):
    wide_count = lax.axis_size("wide")
    narrow_count = lax.axis_size("narrow")
    rows = cells.shape[-2]
    cols = cells.shape[-1]
    above = lax.ppermute(cells[..., rows - width :, :], "wide", shift_pairs(wide_count, 1))
    below = lax.ppermute(cells[..., :width, :], "wide", shift_pairs(wide_count, -1))
    cells = jnp.concatenate([above, cells, below], axis=-2)
    left = lax.ppermute(cells[..., cols - width :], "narrow", shift_pairs(narrow_count, 1))
    right = lax.ppermute(cells[..., :width], "narrow", shift_pairs(narrow_count, -1))
    return jnp.concatenate([left, cells, right], axis=-1)


def plus_halo(cells):
    wide_count = lax.axis_size("wide")
    narrow_count = lax.axis_size("narrow")
    rows = cells.shape[-2]
    cols = cells.shape[-1]
    above = lax.ppermute(cells[:, rows - 1 :, :], "wide", shift_pairs(wide_count, 1))
    below = lax.ppermute(cells[:, :1, :], "wide", shift_pairs(wide_count, -1))
    left = lax.ppermute(cells[:, :, cols - 1], "narrow", shift_pairs(narrow_count, 1))
    right = lax.ppermute(cells[:, :, 0], "narrow", shift_pairs(narrow_count, -1))
    return above, below, left[:, :, None], right[:, :, None]


def column_ranks(owners, peers):
    onehot = (owners[:, None] == jnp.arange(peers, dtype=jnp.int32)[None, :]).astype(jnp.int32)
    before = jnp.cumsum(onehot, axis=0) - onehot
    return jnp.sum(before * onehot, axis=1)


def place_kernel(slots_ref, atm_ref, out_ref):
    tile = out_ref.shape[0]
    columns = slots_ref.shape[1]
    first = pl.program_id(0) * tile
    picked = (
        first + lax.broadcasted_iota(jnp.int32, (tile, columns), 0) == slots_ref[...]
    ).astype(jnp.bfloat16)
    out_ref[...] = lax.dot_general(
        picked,
        atm_ref[...].astype(jnp.bfloat16),
        (((1,), (1,)), ((), ())),
        preferred_element_type=jnp.float32,
    ).astype(out_ref.dtype)


def place_columns(source, slots, total):
    features, columns = source.shape
    tile = min(total, 1024)
    return pl.pallas_call(
        place_kernel,
        out_shape=jax.ShapeDtypeStruct((total, features), jnp.bfloat16),
        grid=(total // tile,),
        in_specs=[
            pl.BlockSpec((1, columns), lambda i: (0, 0)),
            pl.BlockSpec((features, columns), lambda i: (0, 0)),
        ],
        out_specs=pl.BlockSpec((tile, features), lambda i: (i, 0)),
        cost_estimate=pl.CostEstimate(
            flops=2 * total * columns * features,
            transcendentals=0,
            bytes_accessed=4 * features * columns + 2 * total * features,
        ),
    )(slots.reshape(1, columns), source)


def physics_kernel(x_ref, op_ref, fm_ref, out_ref):
    features = x_ref.shape[1]
    initial = x_ref[...].astype(jnp.float32)
    current = initial
    for sweep in range(op_ref.shape[0]):
        mixed = jnp.dot(
            current.astype(jnp.bfloat16), op_ref[sweep], preferred_element_type=jnp.float32
        )
        current = current + relax_rate * jnp.tanh(mixed)
    final = current.astype(jnp.bfloat16)
    out_ref[:, :features] = (current - initial).astype(jnp.bfloat16)
    out_ref[:, features:] = jnp.dot(
        final, fm_ref[...], preferred_element_type=jnp.float32
    ).astype(jnp.bfloat16)


def physics(operators, columns, flux_map):
    slots, features = columns.shape
    nflux = flux_map.shape[1]
    tile = min(slots, 2048)
    sweeps = operators.shape[0]
    return pl.pallas_call(
        physics_kernel,
        out_shape=jax.ShapeDtypeStruct((slots, features + nflux), jnp.bfloat16),
        grid=(slots // tile,),
        in_specs=[
            pl.BlockSpec((tile, features), lambda i: (i, 0)),
            pl.BlockSpec((sweeps, features, features), lambda i: (0, 0, 0)),
            pl.BlockSpec((features, nflux), lambda i: (0, 0)),
        ],
        out_specs=pl.BlockSpec((tile, features + nflux), lambda i: (i, 0)),
        cost_estimate=pl.CostEstimate(
            flops=2 * slots * features * (sweeps * features + nflux),
            transcendentals=sweeps * slots * features,
            bytes_accessed=2 * slots * (2 * features + nflux) + 2 * sweeps * features * features,
        ),
    )(columns, operators, flux_map)


def fetch_kernel(slots_ref, back_ref, atm_ref, atm_out_ref, flux_out_ref):
    features = atm_ref.shape[0]
    count = back_ref.shape[0]
    tile = slots_ref.shape[1]
    picked = (lax.broadcasted_iota(jnp.int32, (count, tile), 0) == slots_ref[...]).astype(
        jnp.bfloat16
    )
    got = lax.dot_general(
        back_ref[...], picked, (((0,), (0,)), ((), ())), preferred_element_type=jnp.float32
    )
    atm_out_ref[...] = atm_ref[...] + got[:features]
    flux_out_ref[...] = got[features:].astype(flux_out_ref.dtype)


def fetch(back, slots, atm_state):
    count, width = back.shape
    features, columns = atm_state.shape
    tile = min(columns, 1024)
    return pl.pallas_call(
        fetch_kernel,
        out_shape=(
            jax.ShapeDtypeStruct((features, columns), jnp.float32),
            jax.ShapeDtypeStruct((width - features, columns), jnp.bfloat16),
        ),
        grid=(columns // tile,),
        in_specs=[
            pl.BlockSpec((1, tile), lambda i: (0, i)),
            pl.BlockSpec((count, width), lambda i: (0, 0)),
            pl.BlockSpec((features, tile), lambda i: (0, i)),
        ],
        out_specs=(
            pl.BlockSpec((features, tile), lambda i: (0, i)),
            pl.BlockSpec((width - features, tile), lambda i: (0, i)),
        ),
        cost_estimate=pl.CostEstimate(
            flops=2 * count * width * columns,
            transcendentals=0,
            bytes_accessed=2 * count * width + 8 * columns * features + 2 * columns * width,
        ),
    )(slots.reshape(1, columns), back, atm_state)


def selector(count, origin, offset, limit, base, size):
    fine = origin + jnp.arange(count, dtype=jnp.int32)
    coarse = jnp.clip(fine // 2 + offset, 0, limit - 1) - base
    return (coarse[:, None] == jnp.arange(size, dtype=jnp.int32)[None, :]).astype(jnp.bfloat16)


def remap(flux_ext, src_ext, weight_ext, ocean_rows, ocean_cols, atm_rows, atm_cols):
    nflux = flux_ext.shape[0]
    ext_r = src_ext.shape[1]
    ext_c = src_ext.shape[2]
    block_r = flux_ext.shape[1] - 2 * ATM_HALO
    block_c = flux_ext.shape[2] - 2 * ATM_HALO
    my_wide = lax.axis_index("wide")
    my_narrow = lax.axis_index("narrow")
    row0 = my_wide * ocean_rows - OCEAN_HALO
    col0 = my_narrow * ocean_cols - OCEAN_HALO
    arow0 = my_wide * block_r - ATM_HALO
    acol0 = my_narrow * block_c - ATM_HALO
    col_sel = jnp.concatenate(
        [
            selector(ext_c, col0, dc, atm_cols, acol0, flux_ext.shape[2]).T
            for dc in (-1, 0, 1)
        ],
        axis=1,
    )
    by_cols = jnp.einsum(
        "fpt,tx->fpx", flux_ext, col_sel, preferred_element_type=jnp.float32
    ).astype(jnp.bfloat16)
    ocean_flux = jnp.zeros((nflux, ext_r, ext_c), jnp.float32)
    for dr in (-1, 0, 1):
        row_sel = selector(ext_r, row0, dr, atm_rows, arow0, flux_ext.shape[1])
        shifted = jnp.einsum(
            "ap,fpx->fax", row_sel, by_cols, preferred_element_type=jnp.float32
        )
        for dc in (-1, 0, 1):
            code = (dr + 1) * 3 + (dc + 1)
            weight_sum = jnp.sum(jnp.where(src_ext == code, weight_ext, 0.0), axis=0)
            window = shifted[:, :, (dc + 1) * ext_c : (dc + 2) * ext_c]
            ocean_flux = ocean_flux + weight_sum[None] * window
    return ocean_flux


def diffuse(centre, above, below, left, right, mask, m_above, m_below, m_left, m_right):
    north = jnp.concatenate([centre[:, 1:, :], below], axis=1)
    south = jnp.concatenate([above, centre[:, :-1, :]], axis=1)
    east = jnp.concatenate([centre[:, :, 1:], right], axis=2)
    west = jnp.concatenate([left, centre[:, :, :-1]], axis=2)
    mn = jnp.concatenate([mask[:, 1:, :], m_below], axis=1)
    ms = jnp.concatenate([m_above, mask[:, :-1, :]], axis=1)
    me = jnp.concatenate([mask[:, :, 1:], m_right], axis=2)
    mw = jnp.concatenate([m_left, mask[:, :, :-1]], axis=2)
    summed = jnp.zeros_like(centre)
    for nb, mb in ((north, mn), (south, ms), (east, me), (west, mw)):
        summed = summed + mask * mb * (nb - centre)
    return centre + kappa_mix * summed


def momentum(flow, height, height_next, mask, mask_next, stress):
    return mask * mask_next * (flow - gravity * (height_next - height) + wind_gain * stress)


def continuity(height, flow_u, flow_u_west, flow_v, flow_v_south, mask, fresh):
    return mask * (
        height - depth_mean * (flow_u - flow_u_west + (flow_v - flow_v_south)) + fresh_gain * fresh
    )


def next_col(x):
    return jnp.concatenate([x[:, 1:], jnp.zeros_like(x[:, :1])], axis=1)


def next_row(x):
    return jnp.concatenate([x[1:, :], jnp.zeros_like(x[:1, :])], axis=0)


def prev_col(x):
    return jnp.concatenate([jnp.zeros_like(x[:, :1]), x[:, :-1]], axis=1)


def prev_row(x):
    return jnp.concatenate([jnp.zeros_like(x[:1, :]), x[:-1, :]], axis=0)


def per_device(
    atm_state,
    group_owner,
    regime_ops,
    flux_map,
    remap_src,
    remap_weight,
    ocean_mask,
    tracer,
    surface_height,
    transports,
):
    peers = lax.axis_size(("wide", "narrow"))
    wide_count = lax.axis_size("wide")
    narrow_count = lax.axis_size("narrow")
    columns_here = atm_state.shape[1]
    nflux = flux_map.shape[1]
    capacity = 2 * columns_here // peers
    total_slots = peers * capacity
    block_rows = columns_here // AC
    ocean_rows = remap_src.shape[1]
    ocean_cols = remap_src.shape[2]
    kk = remap_src.shape[0]
    h = OCEAN_HALO

    mask = ocean_mask.astype(jnp.float32)
    planes = jnp.concatenate(
        [mask[None], surface_height[None], transports, remap_src.astype(jnp.float32), remap_weight],
        axis=0,
    )
    planes_ext = with_halo(planes, h)
    t_above, t_below, t_left, t_right = plus_halo(tracer)
    mask_ext = planes_ext[0]
    m_above = mask_ext[None, h - 1 : h, h:-h]
    m_below = mask_ext[None, h + ocean_rows : h + ocean_rows + 1, h:-h]
    m_left = mask_ext[None, h:-h, h - 1 : h]
    m_right = mask_ext[None, h:-h, h + ocean_cols : h + ocean_cols + 1]
    tracer_mixed = diffuse(
        tracer, t_above, t_below, t_left, t_right, mask[None], m_above, m_below, m_left, m_right
    )

    owners = group_owner[:, 0]
    slots = owners * capacity + column_ranks(owners, peers)
    outgoing = place_columns(atm_state, slots, total_slots)
    arrived = lax.all_to_all(outgoing, ("wide", "narrow"), split_axis=0, concat_axis=0, tiled=True)
    back = lax.all_to_all(
        physics(regime_ops[0], arrived, flux_map),
        ("wide", "narrow"),
        split_axis=0,
        concat_axis=0,
        tiled=True,
    )
    atm_new, flux_cols = fetch(back, slots, atm_state)
    mask_ext = planes_ext[0]
    eta = planes_ext[1]
    flow_u = planes_ext[2]
    flow_v = planes_ext[3]
    src_ext = planes_ext[4 : 4 + kk].astype(jnp.int32)
    weight_ext = planes_ext[4 + kk : 4 + 2 * kk]

    flux_block = flux_cols.astype(jnp.bfloat16).reshape(nflux, block_rows, AC)
    flux_ext = with_halo(flux_block, ATM_HALO)
    ocean_flux = remap(
        flux_ext,
        src_ext,
        weight_ext,
        ocean_rows,
        ocean_cols,
        wide_count * block_rows,
        narrow_count * AC,
    )

    inner = (slice(h, h + ocean_rows), slice(h, h + ocean_cols))
    tracer_new = tracer_mixed.at[0].add(heat_gain * mask * ocean_flux[0][inner])

    mask_east = next_col(mask_ext)
    mask_north = next_row(mask_ext)
    for _ in range(NSUB):
        flow_u = momentum(flow_u, eta, next_col(eta), mask_ext, mask_east, ocean_flux[2])
        flow_v = momentum(flow_v, eta, next_row(eta), mask_ext, mask_north, ocean_flux[3])
        eta = continuity(
            eta, flow_u, prev_col(flow_u), flow_v, prev_row(flow_v), mask_ext, ocean_flux[1]
        )
    return (atm_new, tracer_new, eta[inner], jnp.stack([flow_u[inner], flow_v[inner]]))


def solution(mesh):
    in_specs = (
        P(None, ("wide", "narrow")),
        P(("wide", "narrow"), None),
        P(("wide", "narrow"), None, None, None),
        P(),
        P(None, "wide", "narrow"),
        P(None, "wide", "narrow"),
        P("wide", "narrow"),
        P(None, "wide", "narrow"),
        P("wide", "narrow"),
        P(None, "wide", "narrow"),
    )
    out_specs = (
        P(None, ("wide", "narrow")),
        P(None, "wide", "narrow"),
        P("wide", "narrow"),
        P(None, "wide", "narrow"),
    )

    return jax.shard_map(per_device, mesh=mesh, in_specs=in_specs, out_specs=out_specs, check_vma=False)
```
